256 devices in a mesh: seq: 32 (over z, y_hi, core), tp: 8 (over y_lo, x).
Axes of the slice: x: 4, y: 4 (y_hi: 2, y_lo: 2; y = y_hi * 2 + y_lo), z: 8, core: 2. Of those that a mesh axis runs over, the one named last changes fastest.
Arguments:
- queries: bfloat16 [12288, 3072], P('seq', 'tp'), may hold values from -16 to 16
- keys: bfloat16 [12288, 3072], P('seq', 'tp'), may hold values from -6 to 6
- values: bfloat16 [12288, 3072], P('seq', 'tp'), may hold values from -6 to 6
- resid: bfloat16 [12288, 6144], P(('seq', 'tp')), may hold values from -6 to 6
- out_weight: bfloat16 [3072, 6144], P('tp'), may hold values from -0.109375 to 0.109375
- gain: float32 [6144], replicated, may hold values from 0.1 to 1.9
- pair_of_device: int32 [32], replicated, may hold values from 0 to 31, each once
- frame_of_tile: int32 [64], replicated, may hold values from 0 to 8, as said below
Outputs:
- layer_out: bfloat16 [12288, 6144], P(('seq', 'tp'))
The draws below stay inside these ranges and needn't reach their ends.
Inputs may be any that keep to these rules, and one draw needn't show every extreme that they name: `pair_of_device`: each value once. Frames have equal length, 8 tiles; the sequence starts inside frame 0 and ends inside frame 8, so only these two are partial: frame_of_tile[t] = (t + o) // 8 for an offset o from 1 to 7.
All inputs are finite; a program needn't handle non-finite values.
Results may differ from the reference program's by a relative error of at most 0.025.
Values may be sent and summed in bfloat16 or wider, within the bound.
No kernel may reach another device: no remote copies, remote signals or barrier semaphores. Data moves between devices by JAX's collectives and lax.ppermute only.
A program may use at most 128 MiB of HBM per device.

```python
import math
import jax
import jax.numpy as jnp
from jax import lax

D = 6144
HEADS = 24
HEAD = 128
FRAMES = 8
SPAN = 192
HD = 3072
NCH = 64
TOKENS = 12288
N_SEQ = 32


def draw_queries(key, part):
    return jnp.clip(jax.random.normal(jax.random.fold_in(key, 11), (TOKENS, HD), jnp.float32), -6.0, 6.0).astype(jnp.bfloat16)


def draw_keys(key, part):
    return jnp.clip(jax.random.normal(jax.random.fold_in(key, 13), (TOKENS, HD), jnp.float32), -6.0, 6.0).astype(jnp.bfloat16)


def draw_frame_of_tile(key, part):
    per_frame = NCH // FRAMES
    offset = jax.random.randint(jax.random.fold_in(key, 4242), (), 1, per_frame, dtype=jnp.int32)
    tile_ids = jnp.arange(NCH, dtype=jnp.int32)
    return ((tile_ids + offset) // per_frame).astype(jnp.int32)


def steps_of(rng, extent, pieces, smallest, high):
    def one(position, blocks):
        steps = jax.random.uniform(jax.random.fold_in(jax.random.fold_in(rng, 6), position), (blocks,), jnp.float32, smallest / len(pieces), high / len(pieces))
        return jnp.repeat(jnp.exp(steps), extent[position] // blocks).reshape((-1,) + (1,) * (len(extent) - position - 1))

    loudness = one(*pieces[0])
    for cut in pieces[1:]:
        loudness = loudness * one(*cut)
    return loudness


def gaussian(rng, dims, deviation, most, pieces=(), kind=jnp.bfloat16):
    drawn = deviation * jax.random.normal(rng, dims, jnp.float32)
    if pieces:
        drawn = drawn * steps_of(rng, dims, pieces, -0.22, 0.18)
    return jnp.clip(drawn, -most, most).astype(kind)


def setup_inputs(seed: int = 0) -> dict:
    streams_of = jax.random.split(jax.random.key(seed), 9)
    return {
        "queries": draw_queries(jax.random.fold_in(streams_of[8], 71), 0),
        "keys": draw_keys(jax.random.fold_in(streams_of[8], 71), 0),
        "values": gaussian(streams_of[2], (TOKENS, HD), 1.0, 6.0, ((0, 32), (1, 8))),
        "resid": gaussian(streams_of[3], (TOKENS, D), 1.0, 6.0, ((0, 256),)),
        "out_weight": gaussian(streams_of[4], (HD, D), HD ** -0.5, 0.109375, ((0, 8),)),
        "gain": jnp.clip(1.0 + 0.18 * jax.random.normal(streams_of[5], (D,), jnp.float32), 0.1, 1.9),
        "pair_of_device": jax.random.permutation(streams_of[6], N_SEQ).astype(jnp.int32),
        "frame_of_tile": draw_frame_of_tile(jax.random.fold_in(streams_of[8], 71), 0),
    }


def slot_frames(pair_of_device, frame_of_tile, tile_count):
    slot_ids = jnp.arange(tile_count, dtype=jnp.int32)
    paired = jnp.repeat(pair_of_device, 2)
    tile_ids = jnp.where(slot_ids % 2 == 0, paired, tile_count - 1 - paired)
    matches = tile_ids[:, None] == jnp.arange(tile_count, dtype=jnp.int32)[None, :]
    return lax.optimization_barrier(jnp.sum(jnp.where(matches, frame_of_tile[None, :], 0), axis=1)).astype(jnp.int32)

def reference(queries, keys, values, resid, out_weight, gain, pair_of_device, frame_of_tile):
    slot_frame = slot_frames(pair_of_device, frame_of_tile, NCH)
    row_frame = jnp.repeat(slot_frame, SPAN)
    key_heads = keys.reshape(TOKENS, HEADS, HEAD).astype(jnp.float32)
    value_heads = values.reshape(TOKENS, HEADS, HEAD).astype(jnp.float32)
    score_scale = 1.0 / math.sqrt(HEAD)

    def one_slot(slot):
        first = (slot * SPAN).astype(jnp.int32)
        query_rows = lax.dynamic_slice_in_dim(queries, first, SPAN, 0)
        query_heads = query_rows.reshape(SPAN, HEADS, HEAD).astype(jnp.float32)
        scores = jnp.einsum('qhd,khd->hqk', query_heads, key_heads) * score_scale
        own_frame = lax.dynamic_slice_in_dim(slot_frame, slot.astype(jnp.int32), 1, 0)
        allowed = (row_frame <= own_frame[0])[None, None, :]
        masked = jnp.where(allowed, scores, jnp.float32(-1e+30))
        row_max = lax.optimization_barrier(jnp.max(masked, axis=-1))
        probs = jnp.where(allowed, jnp.exp(masked - row_max[..., None]), jnp.float32(0.0))
        row_totals = lax.optimization_barrier(jnp.sum(probs, axis=-1))
        probs_bf = probs.astype(jnp.bfloat16).astype(jnp.float32)
        weighted = jnp.einsum('hqk,khd->hqd', probs_bf, value_heads)
        attn = weighted / row_totals[..., None]
        return jnp.transpose(attn, (1, 0, 2)).reshape(SPAN, HD).astype(jnp.bfloat16)
    attn = lax.map(one_slot, jnp.arange(NCH, dtype=jnp.int32)).reshape(TOKENS, HD)
    branch = jnp.dot(attn, out_weight, preferred_element_type=jnp.float32)
    rms = jnp.sqrt(lax.optimization_barrier(jnp.mean(branch * branch, axis=-1)) + 1e-06)
    layer_out = resid.astype(jnp.float32) + gain[None, :] * branch / rms[:, None]
    return layer_out.astype(jnp.bfloat16)
```

```python
import functools
import math

import jax
import jax.numpy as jnp
from jax import lax
from jax.experimental import pallas as pl
from jax.experimental.pallas import tpu as pltpu
from jax.sharding import PartitionSpec as P

HEAD = 128
KEY_CHUNK = 1536


def slot_frames(pair_of_device, frame_of_tile, tile_count):
    slot_ids = jnp.arange(tile_count, dtype=jnp.int32)
    paired = jnp.repeat(pair_of_device, 2)
    tile_ids = jnp.where(slot_ids % 2 == 0, paired, tile_count - 1 - paired)
    matches = tile_ids[:, None] == jnp.arange(tile_count, dtype=jnp.int32)[None, :]
    return jnp.sum(jnp.where(matches, frame_of_tile[None, :], 0), axis=1)


def attn_kernel(frame_ref, q_ref, k_ref, v_ref, kf_ref, o_ref, s_sc):
    own_frame = frame_ref[pl.program_id(0)]
    key_count = k_ref.shape[0]
    chunks = key_count // KEY_CHUNK
    rows = q_ref.shape[0]
    score_scale = 1.0 / math.sqrt(HEAD)
    q = q_ref[...]

    def first(c, run_max):
        start = pl.multiple_of(c * KEY_CHUNK, KEY_CHUNK)
        k = k_ref[pl.ds(start, KEY_CHUNK), :]
        s = lax.dot_general(
            q, k, (((1,), (1,)), ((), ())), preferred_element_type=jnp.float32
        ) * score_scale
        allowed = kf_ref[:, pl.ds(start, KEY_CHUNK)] <= own_frame
        masked = jnp.where(allowed, s, jnp.float32(-1e30))
        s_sc[:, pl.ds(start, KEY_CHUNK)] = masked
        return jnp.maximum(run_max, jnp.max(masked, axis=1, keepdims=True))

    row_max = lax.fori_loop(
        0, chunks, first, jnp.full((rows, 1), -1e30, jnp.float32)
    )

    def second(c, carry):
        totals, acc = carry
        start = pl.multiple_of(c * KEY_CHUNK, KEY_CHUNK)
        allowed = kf_ref[:, pl.ds(start, KEY_CHUNK)] <= own_frame
        probs = jnp.where(
            allowed, jnp.exp(s_sc[:, pl.ds(start, KEY_CHUNK)] - row_max), jnp.float32(0.0)
        )
        totals = totals + jnp.sum(probs, axis=1, keepdims=True)
        v = v_ref[pl.ds(start, KEY_CHUNK), :]
        acc = acc + jnp.dot(
            probs.astype(jnp.bfloat16), v, preferred_element_type=jnp.float32
        )
        return totals, acc

    totals, acc = lax.fori_loop(
        0,
        chunks,
        second,
        (jnp.zeros((rows, 1), jnp.float32), jnp.zeros((rows, HEAD), jnp.float32)),
    )
    o_ref[...] = (acc / totals).astype(o_ref.dtype)


def head_attention(own_frames, queries, kv_rows, key_frame, head):
    tok_rows = queries.shape[0]
    tile_rows = tok_rows // 2
    key_count = kv_rows.shape[0]
    cost = pl.CostEstimate(
        flops=4 * tok_rows * key_count * HEAD,
        transcendentals=tok_rows * key_count,
        bytes_accessed=key_count * 2 * HEAD * 2 + tok_rows * HEAD * 4,
    )
    return pl.pallas_call(
        attn_kernel,
        out_shape=jax.ShapeDtypeStruct((tok_rows, HEAD), jnp.bfloat16),
        grid_spec=pltpu.PrefetchScalarGridSpec(
            num_scalar_prefetch=1,
            grid=(2,),
            in_specs=[
                pl.BlockSpec((tile_rows, HEAD), lambda i, fr: (i, head)),
                pl.BlockSpec((key_count, HEAD), lambda i, fr: (0, 0)),
                pl.BlockSpec((key_count, HEAD), lambda i, fr: (0, 1)),
                pl.BlockSpec((1, key_count), lambda i, fr: (0, 0)),
            ],
            out_specs=pl.BlockSpec((tile_rows, HEAD), lambda i, fr: (i, 0)),
            scratch_shapes=[pltpu.VMEM((tile_rows, key_count), jnp.float32)],
        ),
        compiler_params=pltpu.CompilerParams(vmem_limit_bytes=56 * 1024 * 1024),
        cost_estimate=cost,
    )(own_frames, queries, kv_rows, kv_rows, key_frame)


def local(queries, keys, values, resid, out_weight, gain, pair_of_device, frame_of_tile):
    tok_rows, row_width = queries.shape
    head_count = row_width // HEAD
    span_rows = tok_rows // 2
    seq_count = lax.axis_size("seq")
    seq_index = lax.axis_index("seq")
    slot_frame = slot_frames(pair_of_device, frame_of_tile, 2 * seq_count)
    own_frames = lax.dynamic_slice_in_dim(slot_frame, 2 * seq_index, 2, 0).astype(jnp.int32)
    key_frame = jnp.repeat(slot_frame.astype(jnp.int32), span_rows).reshape(1, -1)

    partial = None
    for head in range(head_count):
        cols = slice(head * HEAD, (head + 1) * HEAD)
        kv_local = jnp.concatenate([keys[:, cols], values[:, cols]], axis=1)
        kv_rows = lax.all_gather(kv_local, "seq", axis=0, tiled=True)
        attn_h = head_attention(own_frames, queries, kv_rows, key_frame, head)
        term = jnp.dot(attn_h, out_weight[cols, :], preferred_element_type=jnp.float32)
        partial = term if partial is None else partial + term

    branch = lax.psum_scatter(
        partial.astype(jnp.bfloat16),
        "tp",
        scatter_dimension=0,
        tiled=True,
    ).astype(jnp.float32)
    rms = jnp.sqrt(jnp.mean(branch * branch, axis=-1) + 1e-06)
    layer_out = resid.astype(jnp.float32) + gain[None, :] * branch / rms[:, None]
    return layer_out.astype(jnp.bfloat16)


def solution(mesh):
    in_specs = (
        P("seq", "tp"),
        P("seq", "tp"),
        P("seq", "tp"),
        P(("seq", "tp"), None),
        P("tp", None),
        P(),
        P(),
        P(),
    )
    out_specs = P(("seq", "tp"), None)
    return jax.shard_map(local, mesh=mesh, in_specs=in_specs, out_specs=out_specs, check_vma=False)
```

```python
import functools
import math

import jax
import jax.numpy as jnp
from jax import lax
from jax.experimental import pallas as pl
from jax.experimental.pallas import tpu as pltpu
from jax.sharding import PartitionSpec as P

HEAD = 128
KEY_CHUNK = 1536


def slot_frames(pair_of_device, frame_of_tile, tile_count):
    slot_ids = jnp.arange(tile_count, dtype=jnp.int32)
    paired = jnp.repeat(pair_of_device, 2)
    tile_ids = jnp.where(slot_ids % 2 == 0, paired, tile_count - 1 - paired)
    matches = tile_ids[:, None] == jnp.arange(tile_count, dtype=jnp.int32)[None, :]
    return jnp.sum(jnp.where(matches, frame_of_tile[None, :], 0), axis=1)


def attn_kernel(q_ref, k_ref, v_ref, kf_ref, o_ref, s_sc):
    key_count = k_ref.shape[0]
    chunks = key_count // KEY_CHUNK
    rows = q_ref.shape[0]
    score_scale = 1.0 / math.sqrt(HEAD)
    q = q_ref[...]

    def first(c, run_max):
        start = pl.multiple_of(c * KEY_CHUNK, KEY_CHUNK)
        k = k_ref[pl.ds(start, KEY_CHUNK), :]
        s = lax.dot_general(
            q, k, (((1,), (1,)), ((), ())), preferred_element_type=jnp.float32
        ) * score_scale
        masked = s + kf_ref[:, pl.ds(start, KEY_CHUNK)]
        s_sc[:, pl.ds(start, KEY_CHUNK)] = masked
        return jnp.maximum(run_max, jnp.max(masked, axis=1, keepdims=True))

    row_max = lax.fori_loop(
        0, chunks, first, jnp.full((rows, 1), -1e30, jnp.float32)
    )

    def second(c, carry):
        totals, acc = carry
        start = pl.multiple_of(c * KEY_CHUNK, KEY_CHUNK)
        probs = jnp.exp(s_sc[:, pl.ds(start, KEY_CHUNK)] - row_max)
        totals = totals + jnp.sum(probs, axis=1, keepdims=True)
        v = v_ref[pl.ds(start, KEY_CHUNK), :]
        acc = acc + jnp.dot(
            probs.astype(jnp.bfloat16), v, preferred_element_type=jnp.float32
        )
        return totals, acc

    totals, acc = lax.fori_loop(
        0,
        chunks,
        second,
        (jnp.zeros((rows, 1), jnp.float32), jnp.zeros((rows, HEAD), jnp.float32)),
    )
    o_ref[...] = (acc / totals).astype(o_ref.dtype)


def head_attention(queries, kv_rows, key_bias, head):
    tok_rows = queries.shape[0]
    tile_rows = tok_rows // 2
    key_count = kv_rows.shape[0]
    head_count = queries.shape[1] // HEAD
    cost = pl.CostEstimate(
        flops=4 * tok_rows * key_count * HEAD,
        transcendentals=tok_rows * key_count,
        bytes_accessed=key_count * 2 * HEAD * 2 + tok_rows * HEAD * 4,
    )
    return pl.pallas_call(
        attn_kernel,
        out_shape=jax.ShapeDtypeStruct((tok_rows, HEAD), jnp.bfloat16),
        grid=(2,),
        in_specs=[
            pl.BlockSpec((tile_rows, HEAD), lambda i: (i, head)),
            pl.BlockSpec((key_count, HEAD), lambda i: (0, head)),
            pl.BlockSpec((key_count, HEAD), lambda i: (0, head_count + head)),
            pl.BlockSpec((None, 1, key_count), lambda i: (i, 0, 0)),
        ],
        out_specs=pl.BlockSpec((tile_rows, HEAD), lambda i: (i, 0)),
        scratch_shapes=[pltpu.VMEM((tile_rows, key_count), jnp.float32)],
        compiler_params=pltpu.CompilerParams(vmem_limit_bytes=56 * 1024 * 1024),
        cost_estimate=cost,
    )(queries, kv_rows, kv_rows, key_bias)


def local(queries, keys, values, resid, out_weight, gain, pair_of_device, frame_of_tile):
    tok_rows, row_width = queries.shape
    head_count = row_width // HEAD
    span_rows = tok_rows // 2
    seq_count = lax.axis_size("seq")
    seq_index = lax.axis_index("seq")
    slot_frame = slot_frames(pair_of_device, frame_of_tile, 2 * seq_count)
    own_frames = lax.dynamic_slice_in_dim(slot_frame, 2 * seq_index, 2, 0).astype(jnp.int32)
    key_frame = jnp.repeat(slot_frame.astype(jnp.int32), span_rows)
    key_bias = jnp.where(
        key_frame[None, :] <= own_frames[:, None], jnp.float32(0.0), jnp.float32(-1e30)
    ).reshape(2, 1, -1)

    kv_local = jnp.concatenate([keys, values], axis=1)
    kv_rows = lax.all_gather(kv_local, "seq", axis=0, tiled=True)
    partial = None
    for head in range(head_count):
        cols = slice(head * HEAD, (head + 1) * HEAD)
        attn_h = head_attention(queries, kv_rows, key_bias, head)
        term = jnp.dot(attn_h, out_weight[cols, :], preferred_element_type=jnp.float32)
        partial = term if partial is None else partial + term

    branch = lax.psum_scatter(
        partial.astype(jnp.bfloat16),
        "tp",
        scatter_dimension=0,
        tiled=True,
    ).astype(jnp.float32)
    rms = jnp.sqrt(jnp.mean(branch * branch, axis=-1) + 1e-06)
    layer_out = resid.astype(jnp.float32) + gain[None, :] * branch / rms[:, None]
    return layer_out.astype(jnp.bfloat16)


def solution(mesh):
    in_specs = (
        P("seq", "tp"),
        P("seq", "tp"),
        P("seq", "tp"),
        P(("seq", "tp"), None),
        P("tp", None),
        P(),
        P(),
        P(),
    )
    out_specs = P(("seq", "tp"), None)
    return jax.shard_map(local, mesh=mesh, in_specs=in_specs, out_specs=out_specs, check_vma=False)
```

```python
import functools
import math

import jax
import jax.numpy as jnp
from jax import lax
from jax.experimental import pallas as pl
from jax.experimental.pallas import tpu as pltpu
from jax.sharding import PartitionSpec as P

HEAD = 128
KEY_CHUNK = 1536


def slot_frames(pair_of_device, frame_of_tile, tile_count):
    slot_ids = jnp.arange(tile_count, dtype=jnp.int32)
    paired = jnp.repeat(pair_of_device, 2)
    tile_ids = jnp.where(slot_ids % 2 == 0, paired, tile_count - 1 - paired)
    matches = tile_ids[:, None] == jnp.arange(tile_count, dtype=jnp.int32)[None, :]
    return jnp.sum(jnp.where(matches, frame_of_tile[None, :], 0), axis=1)


def attn_kernel(q_ref, k_ref, v_ref, kf_ref, o_ref, s_sc):
    key_count = k_ref.shape[0]
    chunks = key_count // KEY_CHUNK
    rows = q_ref.shape[0]
    score_scale = 1.0 / math.sqrt(HEAD)
    q = q_ref[...]

    def first(c, run_max):
        start = pl.multiple_of(c * KEY_CHUNK, KEY_CHUNK)
        k = k_ref[pl.ds(start, KEY_CHUNK), :]
        s = lax.dot_general(
            q, k, (((1,), (1,)), ((), ())), preferred_element_type=jnp.float32
        ) * score_scale
        masked = s + kf_ref[:, pl.ds(start, KEY_CHUNK)]
        s_sc[:, pl.ds(start, KEY_CHUNK)] = masked
        return jnp.maximum(run_max, jnp.max(masked, axis=1, keepdims=True))

    row_max = lax.fori_loop(
        0, chunks, first, jnp.full((rows, 1), -1e30, jnp.float32)
    )

    def second(c, carry):
        totals, acc = carry
        start = pl.multiple_of(c * KEY_CHUNK, KEY_CHUNK)
        probs = jnp.exp(s_sc[:, pl.ds(start, KEY_CHUNK)] - row_max)
        totals = totals + jnp.sum(probs, axis=1, keepdims=True)
        v = v_ref[pl.ds(start, KEY_CHUNK), :]
        acc = acc + jnp.dot(
            probs.astype(jnp.bfloat16), v, preferred_element_type=jnp.float32
        )
        return totals, acc

    totals, acc = lax.fori_loop(
        0,
        chunks,
        second,
        (jnp.zeros((rows, 1), jnp.float32), jnp.zeros((rows, HEAD), jnp.float32)),
    )
    o_ref[...] = (acc / totals).astype(o_ref.dtype)


def attention(queries, kv_rows, key_bias):
    tok_rows = queries.shape[0]
    tile_rows = tok_rows // 2
    key_count = kv_rows.shape[0]
    head_count = queries.shape[1] // HEAD
    cost = pl.CostEstimate(
        flops=4 * tok_rows * key_count * HEAD * head_count,
        transcendentals=tok_rows * key_count * head_count,
        bytes_accessed=(key_count * 2 * HEAD * 2 + tok_rows * HEAD * 4) * head_count,
    )
    return pl.pallas_call(
        attn_kernel,
        out_shape=jax.ShapeDtypeStruct((tok_rows, head_count * HEAD), jnp.bfloat16),
        grid=(head_count, 2),
        in_specs=[
            pl.BlockSpec((tile_rows, HEAD), lambda h, i: (i, h)),
            pl.BlockSpec((key_count, HEAD), lambda h, i: (0, h)),
            pl.BlockSpec((key_count, HEAD), lambda h, i: (0, head_count + h)),
            pl.BlockSpec((None, 1, key_count), lambda h, i: (i, 0, 0)),
        ],
        out_specs=pl.BlockSpec((tile_rows, HEAD), lambda h, i: (i, h)),
        scratch_shapes=[pltpu.VMEM((tile_rows, key_count), jnp.float32)],
        compiler_params=pltpu.CompilerParams(vmem_limit_bytes=56 * 1024 * 1024),
        cost_estimate=cost,
    )(queries, kv_rows, kv_rows, key_bias)


def local(queries, keys, values, resid, out_weight, gain, pair_of_device, frame_of_tile):
    tok_rows, row_width = queries.shape
    head_count = row_width // HEAD
    span_rows = tok_rows // 2
    seq_count = lax.axis_size("seq")
    seq_index = lax.axis_index("seq")
    slot_frame = slot_frames(pair_of_device, frame_of_tile, 2 * seq_count)
    own_frames = lax.dynamic_slice_in_dim(slot_frame, 2 * seq_index, 2, 0).astype(jnp.int32)
    key_frame = jnp.repeat(slot_frame.astype(jnp.int32), span_rows)
    key_bias = jnp.where(
        key_frame[None, :] <= own_frames[:, None], jnp.float32(0.0), jnp.float32(-1e30)
    ).reshape(2, 1, -1)

    kv_local = jnp.concatenate([keys, values], axis=1)
    kv_rows = lax.all_gather(kv_local, "seq", axis=0, tiled=True)
    attn = attention(queries, kv_rows, key_bias)
    partial = jnp.dot(attn, out_weight, preferred_element_type=jnp.float32)

    branch = lax.psum_scatter(
        partial.astype(jnp.bfloat16),
        "tp",
        scatter_dimension=0,
        tiled=True,
    ).astype(jnp.float32)
    rms = jnp.sqrt(jnp.mean(branch * branch, axis=-1) + 1e-06)
    layer_out = resid.astype(jnp.float32) + gain[None, :] * branch / rms[:, None]
    return layer_out.astype(jnp.bfloat16)


def solution(mesh):
    in_specs = (
        P("seq", "tp"),
        P("seq", "tp"),
        P("seq", "tp"),
        P(("seq", "tp"), None),
        P("tp", None),
        P(),
        P(),
        P(),
    )
    out_specs = P(("seq", "tp"), None)
    return jax.shard_map(local, mesh=mesh, in_specs=in_specs, out_specs=out_specs, check_vma=False)
```

```python
import functools
import math

import jax
import jax.numpy as jnp
from jax import lax
from jax.experimental import pallas as pl
from jax.experimental.pallas import tpu as pltpu
from jax.sharding import PartitionSpec as P

HEAD = 128


def slot_frames(pair_of_device, frame_of_tile, tile_count):
    slot_ids = jnp.arange(tile_count, dtype=jnp.int32)
    paired = jnp.repeat(pair_of_device, 2)
    tile_ids = jnp.where(slot_ids % 2 == 0, paired, tile_count - 1 - paired)
    matches = tile_ids[:, None] == jnp.arange(tile_count, dtype=jnp.int32)[None, :]
    return jnp.sum(jnp.where(matches, frame_of_tile[None, :], 0), axis=1)


def attn_kernel(order_ref, count_ref, q_ref, k_ref, v_ref, o_ref, s_sc):
    tile = pl.program_id(1)
    visible = count_ref[tile]
    rows = q_ref.shape[0]
    span = s_sc.shape[1]
    score_scale = 1.0 / math.sqrt(HEAD)
    q = q_ref[...]

    def first(j, run_max):
        slot = order_ref[tile, j]
        start = pl.multiple_of(slot * span, span)
        k = k_ref[pl.ds(start, span), :]
        s = lax.dot_general(
            q, k, (((1,), (1,)), ((), ())), preferred_element_type=jnp.float32
        ) * score_scale
        s_sc[j] = s
        return jnp.maximum(run_max, jnp.max(s, axis=1, keepdims=True))

    row_max = lax.fori_loop(0, visible, first, jnp.full((rows, 1), -1e30, jnp.float32))

    def second(j, carry):
        totals, acc = carry
        slot = order_ref[tile, j]
        start = pl.multiple_of(slot * span, span)
        probs = jnp.exp(s_sc[j] - row_max)
        totals = totals + jnp.sum(probs, axis=1, keepdims=True)
        v = v_ref[pl.ds(start, span), :]
        acc = acc + jnp.dot(probs.astype(jnp.bfloat16), v, preferred_element_type=jnp.float32)
        return totals, acc

    totals, acc = lax.fori_loop(
        0,
        visible,
        second,
        (jnp.zeros((rows, 1), jnp.float32), jnp.zeros((rows, HEAD), jnp.float32)),
    )
    o_ref[...] = (acc / totals).astype(o_ref.dtype)


def attention(queries, kv_rows, order, count):
    tok_rows = queries.shape[0]
    tile_rows = tok_rows // 2
    key_count = kv_rows.shape[0]
    head_count = queries.shape[1] // HEAD
    slot_count = order.shape[1]
    span = key_count // slot_count
    cost = pl.CostEstimate(
        flops=2 * tok_rows * key_count * HEAD * head_count,
        transcendentals=tok_rows * key_count * head_count // 2,
        bytes_accessed=(key_count * 2 * HEAD * 2 + tok_rows * HEAD * 4) * head_count,
    )
    return pl.pallas_call(
        attn_kernel,
        out_shape=jax.ShapeDtypeStruct((tok_rows, head_count * HEAD), jnp.bfloat16),
        grid_spec=pltpu.PrefetchScalarGridSpec(
            num_scalar_prefetch=2,
            grid=(head_count, 2),
            in_specs=[
                pl.BlockSpec((tile_rows, HEAD), lambda h, i, o, c: (i, h)),
                pl.BlockSpec((key_count, HEAD), lambda h, i, o, c: (0, h)),
                pl.BlockSpec((key_count, HEAD), lambda h, i, o, c: (0, head_count + h)),
            ],
            out_specs=pl.BlockSpec((tile_rows, HEAD), lambda h, i, o, c: (i, h)),
            scratch_shapes=[pltpu.VMEM((slot_count, tile_rows, span), jnp.float32)],
        ),
        compiler_params=pltpu.CompilerParams(vmem_limit_bytes=56 * 1024 * 1024),
        cost_estimate=cost,
    )(order, count, queries, kv_rows, kv_rows)


def local(queries, keys, values, resid, out_weight, gain, pair_of_device, frame_of_tile):
    tok_rows, row_width = queries.shape
    head_count = row_width // HEAD
    span_rows = tok_rows // 2
    seq_count = lax.axis_size("seq")
    seq_index = lax.axis_index("seq")
    slot_frame = slot_frames(pair_of_device, frame_of_tile, 2 * seq_count)
    own_frames = lax.dynamic_slice_in_dim(slot_frame, 2 * seq_index, 2, 0).astype(jnp.int32)
    slot_count = slot_frame.shape[0]
    slot_ids = jnp.arange(slot_count, dtype=jnp.int32)
    allowed = (slot_frame[None, :] <= own_frames[:, None]).astype(jnp.int32)
    count = jnp.sum(allowed, axis=1).astype(jnp.int32)
    place = jnp.where(
        allowed == 1,
        jnp.cumsum(allowed, axis=1) - 1,
        count[:, None] + jnp.cumsum(1 - allowed, axis=1) - 1,
    )
    order = jnp.sum(
        jnp.where(place[:, :, None] == slot_ids[None, None, :], slot_ids[None, :, None], 0),
        axis=1,
    ).astype(jnp.int32)

    kv_local = jnp.concatenate([keys, values], axis=1)
    kv_rows = lax.all_gather(kv_local, "seq", axis=0, tiled=True)
    attn = attention(queries, kv_rows, order, count)
    partial = jnp.dot(attn, out_weight, preferred_element_type=jnp.float32)

    branch = lax.psum_scatter(
        partial.astype(jnp.bfloat16),
        "tp",
        scatter_dimension=0,
        tiled=True,
    ).astype(jnp.float32)
    rms = jnp.sqrt(jnp.mean(branch * branch, axis=-1) + 1e-06)
    layer_out = resid.astype(jnp.float32) + gain[None, :] * branch / rms[:, None]
    return layer_out.astype(jnp.bfloat16)


def solution(mesh):
    in_specs = (
        P("seq", "tp"),
        P("seq", "tp"),
        P("seq", "tp"),
        P(("seq", "tp"), None),
        P("tp", None),
        P(),
        P(),
        P(),
    )
    out_specs = P(("seq", "tp"), None)
    return jax.shard_map(local, mesh=mesh, in_specs=in_specs, out_specs=out_specs, check_vma=False)
```

```python
import functools
import math

import jax
import jax.numpy as jnp
from jax import lax
from jax.experimental import pallas as pl
from jax.experimental.pallas import tpu as pltpu
from jax.sharding import PartitionSpec as P

HEAD = 128
KEY_CHUNK = 1536


def slot_frames(pair_of_device, frame_of_tile, tile_count):
    slot_ids = jnp.arange(tile_count, dtype=jnp.int32)
    paired = jnp.repeat(pair_of_device, 2)
    tile_ids = jnp.where(slot_ids % 2 == 0, paired, tile_count - 1 - paired)
    matches = tile_ids[:, None] == jnp.arange(tile_count, dtype=jnp.int32)[None, :]
    return jnp.sum(jnp.where(matches, frame_of_tile[None, :], 0), axis=1)


def attn_kernel(q_ref, k_ref, v_ref, kf_ref, o_ref, s_sc):
    key_count = k_ref.shape[0]
    chunks = key_count // KEY_CHUNK
    rows = q_ref.shape[0]
    score_scale = 1.0 / math.sqrt(HEAD)
    q = q_ref[...]

    def first(c, run_max):
        start = pl.multiple_of(c * KEY_CHUNK, KEY_CHUNK)
        k = k_ref[pl.ds(start, KEY_CHUNK), :]
        s = lax.dot_general(
            q, k, (((1,), (1,)), ((), ())), preferred_element_type=jnp.float32
        ) * score_scale
        masked = s + kf_ref[:, pl.ds(start, KEY_CHUNK)]
        s_sc[:, pl.ds(start, KEY_CHUNK)] = masked
        return jnp.maximum(run_max, jnp.max(masked, axis=1, keepdims=True))

    row_max = lax.fori_loop(
        0, chunks, first, jnp.full((rows, 1), -1e30, jnp.float32)
    )

    def second(c, carry):
        totals, acc = carry
        start = pl.multiple_of(c * KEY_CHUNK, KEY_CHUNK)
        probs = jnp.exp(s_sc[:, pl.ds(start, KEY_CHUNK)] - row_max)
        totals = totals + jnp.sum(probs, axis=1, keepdims=True)
        v = v_ref[pl.ds(start, KEY_CHUNK), :]
        acc = acc + jnp.dot(
            probs.astype(jnp.bfloat16), v, preferred_element_type=jnp.float32
        )
        return totals, acc

    totals, acc = lax.fori_loop(
        0,
        chunks,
        second,
        (jnp.zeros((rows, 1), jnp.float32), jnp.zeros((rows, HEAD), jnp.float32)),
    )
    o_ref[...] = (acc / totals).astype(o_ref.dtype)


def attention(queries, kv_rows, key_bias):
    tok_rows = queries.shape[0]
    tile_rows = tok_rows // 2
    key_count = kv_rows.shape[0]
    head_count = queries.shape[1] // HEAD
    cost = pl.CostEstimate(
        flops=4 * tok_rows * key_count * HEAD * head_count,
        transcendentals=tok_rows * key_count * head_count,
        bytes_accessed=(key_count * 2 * HEAD * 2 + tok_rows * HEAD * 4) * head_count,
    )
    return pl.pallas_call(
        attn_kernel,
        out_shape=jax.ShapeDtypeStruct((tok_rows, head_count * HEAD), jnp.bfloat16),
        grid=(head_count, 2),
        in_specs=[
            pl.BlockSpec((tile_rows, HEAD), lambda h, i: (i, h)),
            pl.BlockSpec((key_count, HEAD), lambda h, i: (0, h)),
            pl.BlockSpec((key_count, HEAD), lambda h, i: (0, head_count + h)),
            pl.BlockSpec((None, 1, key_count), lambda h, i: (i, 0, 0)),
        ],
        out_specs=pl.BlockSpec((tile_rows, HEAD), lambda h, i: (i, h)),
        scratch_shapes=[pltpu.VMEM((tile_rows, key_count), jnp.float32)],
        compiler_params=pltpu.CompilerParams(vmem_limit_bytes=56 * 1024 * 1024),
        cost_estimate=cost,
    )(queries, kv_rows, kv_rows, key_bias)


def local(queries, keys, values, resid, out_weight, gain, pair_of_device, frame_of_tile):
    tok_rows, row_width = queries.shape
    head_count = row_width // HEAD
    span_rows = tok_rows // 2
    seq_count = lax.axis_size("seq")
    seq_index = lax.axis_index("seq")
    slot_frame = slot_frames(pair_of_device, frame_of_tile, 2 * seq_count)
    own_frames = lax.dynamic_slice_in_dim(slot_frame, 2 * seq_index, 2, 0).astype(jnp.int32)
    key_frame = jnp.repeat(slot_frame.astype(jnp.int32), span_rows)
    key_bias = jnp.where(
        key_frame[None, :] <= own_frames[:, None], jnp.float32(0.0), jnp.float32(-1e30)
    ).reshape(2, 1, -1)

    kv_local = jnp.concatenate([keys, values], axis=1)
    kv_rows = lax.all_gather(kv_local, "seq", axis=0, tiled=True)
    attn = attention(queries, kv_rows, key_bias)
    partial = jnp.dot(attn, out_weight, preferred_element_type=jnp.float32)

    tp_count = lax.axis_size("tp")
    shares = lax.all_to_all(
        partial.astype(jnp.bfloat16).reshape(tp_count, tok_rows // tp_count, -1),
        "tp",
        0,
        0,
        tiled=False,
    )
    branch = jnp.sum(shares.astype(jnp.float32), axis=0)
    rms = jnp.sqrt(jnp.mean(branch * branch, axis=-1) + 1e-06)
    layer_out = resid.astype(jnp.float32) + gain[None, :] * branch / rms[:, None]
    return layer_out.astype(jnp.bfloat16)


def solution(mesh):
    in_specs = (
        P("seq", "tp"),
        P("seq", "tp"),
        P("seq", "tp"),
        P(("seq", "tp"), None),
        P("tp", None),
        P(),
        P(),
        P(),
    )
    out_specs = P(("seq", "tp"), None)
    return jax.shard_map(local, mesh=mesh, in_specs=in_specs, out_specs=out_specs, check_vma=False)
```

```python
import functools
import math

import jax
import jax.numpy as jnp
from jax import lax
from jax.experimental import pallas as pl
from jax.experimental.pallas import tpu as pltpu
from jax.sharding import PartitionSpec as P

HEAD = 128
SLOTS_PER_CHUNK = 8


def slot_frames(pair_of_device, frame_of_tile, tile_count):
    slot_ids = jnp.arange(tile_count, dtype=jnp.int32)
    paired = jnp.repeat(pair_of_device, 2)
    tile_ids = jnp.where(slot_ids % 2 == 0, paired, tile_count - 1 - paired)
    matches = tile_ids[:, None] == jnp.arange(tile_count, dtype=jnp.int32)[None, :]
    return jnp.sum(jnp.where(matches, frame_of_tile[None, :], 0), axis=1)


def attn_kernel(order_ref, chunks_ref, q_ref, k_ref, v_ref, kb_ref, o_ref, s_sc):
    tile = pl.program_id(1)
    visible = chunks_ref[tile]
    rows = q_ref.shape[0]
    span = k_ref.shape[0] // order_ref.shape[0]
    width = span * SLOTS_PER_CHUNK
    score_scale = 1.0 / math.sqrt(HEAD)
    q = q_ref[...]

    def gather(ref, c):
        pieces = []
        for m in range(SLOTS_PER_CHUNK):
            slot = order_ref[c * SLOTS_PER_CHUNK + m]
            pieces.append(ref[pl.ds(pl.multiple_of(slot * span, span), span), :])
        return jnp.concatenate(pieces, axis=0)

    def first(c, run_max):
        start = pl.multiple_of(c * width, width)
        k = gather(k_ref, c)
        s = lax.dot_general(
            q, k, (((1,), (1,)), ((), ())), preferred_element_type=jnp.float32
        ) * score_scale
        masked = s + kb_ref[:, pl.ds(start, width)]
        s_sc[:, pl.ds(start, width)] = masked
        return jnp.maximum(run_max, jnp.max(masked, axis=1, keepdims=True))

    row_max = lax.fori_loop(0, visible, first, jnp.full((rows, 1), -1e30, jnp.float32))

    def second(c, carry):
        totals, acc = carry
        start = pl.multiple_of(c * width, width)
        probs = jnp.exp(s_sc[:, pl.ds(start, width)] - row_max)
        totals = totals + jnp.sum(probs, axis=1, keepdims=True)
        v = gather(v_ref, c)
        acc = acc + jnp.dot(probs.astype(jnp.bfloat16), v, preferred_element_type=jnp.float32)
        return totals, acc

    totals, acc = lax.fori_loop(
        0,
        visible,
        second,
        (jnp.zeros((rows, 1), jnp.float32), jnp.zeros((rows, HEAD), jnp.float32)),
    )
    o_ref[...] = (acc / totals).astype(o_ref.dtype)


def attention(queries, kv_rows, order, chunks, key_bias):
    tok_rows = queries.shape[0]
    tile_rows = tok_rows // 2
    key_count = kv_rows.shape[0]
    head_count = queries.shape[1] // HEAD
    cost = pl.CostEstimate(
        flops=2 * tok_rows * key_count * HEAD * head_count,
        transcendentals=tok_rows * key_count * head_count // 2,
        bytes_accessed=(key_count * 2 * HEAD * 2 + tok_rows * HEAD * 4) * head_count,
    )
    return pl.pallas_call(
        attn_kernel,
        out_shape=jax.ShapeDtypeStruct((tok_rows, head_count * HEAD), jnp.bfloat16),
        grid_spec=pltpu.PrefetchScalarGridSpec(
            num_scalar_prefetch=2,
            grid=(head_count, 2),
            in_specs=[
                pl.BlockSpec((tile_rows, HEAD), lambda h, i, o, c: (i, h)),
                pl.BlockSpec((key_count, HEAD), lambda h, i, o, c: (0, h)),
                pl.BlockSpec((key_count, HEAD), lambda h, i, o, c: (0, head_count + h)),
                pl.BlockSpec((None, 1, key_count), lambda h, i, o, c: (i, 0, 0)),
            ],
            out_specs=pl.BlockSpec((tile_rows, HEAD), lambda h, i, o, c: (i, h)),
            scratch_shapes=[pltpu.VMEM((tile_rows, key_count), jnp.float32)],
        ),
        compiler_params=pltpu.CompilerParams(vmem_limit_bytes=56 * 1024 * 1024),
        cost_estimate=cost,
    )(order, chunks, queries, kv_rows, kv_rows, key_bias)


def local(queries, keys, values, resid, out_weight, gain, pair_of_device, frame_of_tile):
    tok_rows, row_width = queries.shape
    head_count = row_width // HEAD
    span_rows = tok_rows // 2
    seq_count = lax.axis_size("seq")
    seq_index = lax.axis_index("seq")
    slot_frame = slot_frames(pair_of_device, frame_of_tile, 2 * seq_count)
    own_frames = lax.dynamic_slice_in_dim(slot_frame, 2 * seq_index, 2, 0).astype(jnp.int32)
    slot_count = slot_frame.shape[0]
    slot_ids = jnp.arange(slot_count, dtype=jnp.int32)
    earlier = (slot_frame[None, :] < slot_frame[:, None]) | (
        (slot_frame[None, :] == slot_frame[:, None]) & (slot_ids[None, :] < slot_ids[:, None])
    )
    rank = jnp.sum(earlier.astype(jnp.int32), axis=1)
    order = jnp.sum(
        jnp.where(rank[:, None] == slot_ids[None, :], slot_ids[:, None], 0), axis=0
    ).astype(jnp.int32)
    sorted_frame = jnp.sum(
        jnp.where(rank[:, None] == slot_ids[None, :], slot_frame[:, None], 0), axis=0
    )
    visible = jnp.sum((slot_frame[None, :] <= own_frames[:, None]).astype(jnp.int32), axis=1)
    chunks = ((visible + SLOTS_PER_CHUNK - 1) // SLOTS_PER_CHUNK).astype(jnp.int32)
    key_frame = jnp.repeat(sorted_frame.astype(jnp.int32), span_rows)
    key_bias = jnp.where(
        key_frame[None, :] <= own_frames[:, None], jnp.float32(0.0), jnp.float32(-1e30)
    ).reshape(2, 1, -1)

    kv_local = jnp.concatenate([keys, values], axis=1)
    kv_rows = lax.all_gather(kv_local, "seq", axis=0, tiled=True)
    attn = attention(queries, kv_rows, order, chunks, key_bias)
    partial = jnp.dot(attn, out_weight, preferred_element_type=jnp.float32)

    tp_count = lax.axis_size("tp")
    shares = lax.all_to_all(
        partial.astype(jnp.bfloat16).reshape(tp_count, tok_rows // tp_count, -1),
        "tp",
        0,
        0,
        tiled=False,
    )
    branch = jnp.sum(shares.astype(jnp.float32), axis=0)
    rms = jnp.sqrt(jnp.mean(branch * branch, axis=-1) + 1e-06)
    layer_out = resid.astype(jnp.float32) + gain[None, :] * branch / rms[:, None]
    return layer_out.astype(jnp.bfloat16)


def solution(mesh):
    in_specs = (
        P("seq", "tp"),
        P("seq", "tp"),
        P("seq", "tp"),
        P(("seq", "tp"), None),
        P("tp", None),
        P(),
        P(),
        P(),
    )
    out_specs = P(("seq", "tp"), None)
    return jax.shard_map(local, mesh=mesh, in_specs=in_specs, out_specs=out_specs, check_vma=False)
```

```python
import functools
import math

import jax
import jax.numpy as jnp
from jax import lax
from jax.experimental import pallas as pl
from jax.experimental.pallas import tpu as pltpu
from jax.sharding import PartitionSpec as P

HEAD = 128
SLOTS_PER_CHUNK = 8


def slot_frames(pair_of_device, frame_of_tile, tile_count):
    slot_ids = jnp.arange(tile_count, dtype=jnp.int32)
    paired = jnp.repeat(pair_of_device, 2)
    tile_ids = jnp.where(slot_ids % 2 == 0, paired, tile_count - 1 - paired)
    matches = tile_ids[:, None] == jnp.arange(tile_count, dtype=jnp.int32)[None, :]
    return jnp.sum(jnp.where(matches, frame_of_tile[None, :], 0), axis=1)


def attn_kernel(order_ref, chunks_ref, q_ref, k_ref, v_ref, kb_ref, o_ref, s_sc):
    tile = pl.program_id(1)
    visible = chunks_ref[tile]
    rows = q_ref.shape[0]
    span = k_ref.shape[0] // order_ref.shape[0]
    width = span * SLOTS_PER_CHUNK
    score_scale = 1.0 / math.sqrt(HEAD)
    q = q_ref[...]

    def gather(ref, c):
        pieces = []
        for m in range(SLOTS_PER_CHUNK):
            slot = order_ref[c * SLOTS_PER_CHUNK + m]
            pieces.append(ref[pl.ds(pl.multiple_of(slot * span, span), span), :])
        return jnp.concatenate(pieces, axis=0)

    def first(c, run_max):
        start = pl.multiple_of(c * width, width)
        k = gather(k_ref, c)
        s = lax.dot_general(
            q, k, (((1,), (1,)), ((), ())), preferred_element_type=jnp.float32
        ) * score_scale
        masked = s + kb_ref[:, pl.ds(start, width)]
        s_sc[:, pl.ds(start, width)] = masked
        return jnp.maximum(run_max, jnp.max(masked, axis=1, keepdims=True))

    row_max = lax.fori_loop(0, visible, first, jnp.full((rows, 1), -1e30, jnp.float32))

    def second(c, carry):
        totals, acc = carry
        start = pl.multiple_of(c * width, width)
        probs = jnp.exp(s_sc[:, pl.ds(start, width)] - row_max)
        totals = totals + jnp.sum(probs, axis=1, keepdims=True)
        v = gather(v_ref, c)
        acc = acc + jnp.dot(probs.astype(jnp.bfloat16), v, preferred_element_type=jnp.float32)
        return totals, acc

    totals, acc = lax.fori_loop(
        0,
        visible,
        second,
        (jnp.zeros((rows, 1), jnp.float32), jnp.zeros((rows, HEAD), jnp.float32)),
    )
    o_ref[...] = (acc / totals).astype(o_ref.dtype)


def attention(queries, kv_rows, order, chunks, key_bias):
    tok_rows = queries.shape[0]
    tile_rows = tok_rows // 2
    key_count = kv_rows.shape[0]
    head_count = queries.shape[1] // HEAD
    cost = pl.CostEstimate(
        flops=2 * tok_rows * key_count * HEAD * head_count,
        transcendentals=tok_rows * key_count * head_count // 2,
        bytes_accessed=(key_count * 2 * HEAD * 2 + tok_rows * HEAD * 4) * head_count,
    )
    return pl.pallas_call(
        attn_kernel,
        out_shape=jax.ShapeDtypeStruct((tok_rows, head_count * HEAD), jnp.bfloat16),
        grid_spec=pltpu.PrefetchScalarGridSpec(
            num_scalar_prefetch=2,
            grid=(head_count, 2),
            in_specs=[
                pl.BlockSpec((tile_rows, HEAD), lambda h, i, o, c: (i, h)),
                pl.BlockSpec((key_count, HEAD), lambda h, i, o, c: (0, h)),
                pl.BlockSpec((key_count, HEAD), lambda h, i, o, c: (0, head_count + h)),
                pl.BlockSpec((None, 1, key_count), lambda h, i, o, c: (i, 0, 0)),
            ],
            out_specs=pl.BlockSpec((tile_rows, HEAD), lambda h, i, o, c: (i, h)),
            scratch_shapes=[pltpu.VMEM((tile_rows, key_count), jnp.float32)],
        ),
        compiler_params=pltpu.CompilerParams(vmem_limit_bytes=56 * 1024 * 1024),
        cost_estimate=cost,
    )(order, chunks, queries, kv_rows, kv_rows, key_bias)


def local(queries, keys, values, resid, out_weight, gain, pair_of_device, frame_of_tile):
    tok_rows, row_width = queries.shape
    head_count = row_width // HEAD
    span_rows = tok_rows // 2
    seq_count = lax.axis_size("seq")
    seq_index = lax.axis_index("seq")
    slot_frame = slot_frames(pair_of_device, frame_of_tile, 2 * seq_count)
    own_frames = lax.dynamic_slice_in_dim(slot_frame, 2 * seq_index, 2, 0).astype(jnp.int32)
    slot_count = slot_frame.shape[0]
    slot_ids = jnp.arange(slot_count, dtype=jnp.int32)
    earlier = (slot_frame[None, :] < slot_frame[:, None]) | (
        (slot_frame[None, :] == slot_frame[:, None]) & (slot_ids[None, :] < slot_ids[:, None])
    )
    rank = jnp.sum(earlier.astype(jnp.int32), axis=1)
    order = jnp.sum(
        jnp.where(rank[:, None] == slot_ids[None, :], slot_ids[:, None], 0), axis=0
    ).astype(jnp.int32)
    sorted_frame = jnp.sum(
        jnp.where(rank[:, None] == slot_ids[None, :], slot_frame[:, None], 0), axis=0
    )
    visible = jnp.sum((slot_frame[None, :] <= own_frames[:, None]).astype(jnp.int32), axis=1)
    chunks = ((visible + SLOTS_PER_CHUNK - 1) // SLOTS_PER_CHUNK).astype(jnp.int32)
    key_frame = jnp.repeat(sorted_frame.astype(jnp.int32), span_rows)
    key_bias = jnp.where(
        key_frame[None, :] <= own_frames[:, None], jnp.float32(0.0), jnp.float32(-1e30)
    ).reshape(2, 1, -1)

    kv_local = jnp.concatenate([keys, values], axis=1)
    kv_rows = lax.all_gather(kv_local, "seq", axis=0, tiled=True)
    attn = attention(queries, kv_rows, order, chunks, key_bias)
    tp_count = lax.axis_size("tp")
    share_rows = tok_rows // tp_count
    split = out_weight.shape[1] // 2
    part_a = jnp.dot(attn, out_weight[:, :split], preferred_element_type=jnp.float32)
    branch_a = lax.psum_scatter(
        part_a.astype(jnp.bfloat16), "tp", scatter_dimension=0, tiled=True
    ).astype(jnp.float32)
    part_b = jnp.dot(attn, out_weight[:, split:], preferred_element_type=jnp.float32)
    shares = lax.all_to_all(
        part_b.astype(jnp.bfloat16).reshape(tp_count, share_rows, -1), "tp", 0, 0, tiled=False
    )
    branch_b = jnp.sum(shares.astype(jnp.float32), axis=0)
    branch = jnp.concatenate([branch_a, branch_b], axis=1)
    rms = jnp.sqrt(jnp.mean(branch * branch, axis=-1) + 1e-06)
    layer_out = resid.astype(jnp.float32) + gain[None, :] * branch / rms[:, None]
    return layer_out.astype(jnp.bfloat16)


def solution(mesh):
    in_specs = (
        P("seq", "tp"),
        P("seq", "tp"),
        P("seq", "tp"),
        P(("seq", "tp"), None),
        P("tp", None),
        P(),
        P(),
        P(),
    )
    out_specs = P(("seq", "tp"), None)
    return jax.shard_map(local, mesh=mesh, in_specs=in_specs, out_specs=out_specs, check_vma=False)
```

```python
import functools
import math

import jax
import jax.numpy as jnp
from jax import lax
from jax.experimental import pallas as pl
from jax.experimental.pallas import tpu as pltpu
from jax.sharding import PartitionSpec as P

HEAD = 128
SLOTS_PER_CHUNK = 8


def slot_frames(pair_of_device, frame_of_tile, tile_count):
    slot_ids = jnp.arange(tile_count, dtype=jnp.int32)
    paired = jnp.repeat(pair_of_device, 2)
    tile_ids = jnp.where(slot_ids % 2 == 0, paired, tile_count - 1 - paired)
    matches = tile_ids[:, None] == jnp.arange(tile_count, dtype=jnp.int32)[None, :]
    return jnp.sum(jnp.where(matches, frame_of_tile[None, :], 0), axis=1)


def attn_kernel(order_ref, chunks_ref, q_ref, k_ref, v_ref, kb_ref, o_ref, s_sc):
    visible = chunks_ref[0]
    rows = q_ref.shape[0]
    span = k_ref.shape[0] // order_ref.shape[0]
    width = span * SLOTS_PER_CHUNK
    score_scale = 1.0 / math.sqrt(HEAD)
    q = q_ref[...]

    def gather(ref, c):
        pieces = []
        for m in range(SLOTS_PER_CHUNK):
            slot = order_ref[c * SLOTS_PER_CHUNK + m]
            pieces.append(ref[pl.ds(pl.multiple_of(slot * span, span), span), :])
        return jnp.concatenate(pieces, axis=0)

    def first(c, run_max):
        start = pl.multiple_of(c * width, width)
        k = gather(k_ref, c)
        s = lax.dot_general(
            q, k, (((1,), (1,)), ((), ())), preferred_element_type=jnp.float32
        ) * score_scale
        masked = s + kb_ref[:, pl.ds(start, width)]
        s_sc[:, pl.ds(start, width)] = masked
        return jnp.maximum(run_max, jnp.max(masked, axis=1, keepdims=True))

    row_max = lax.fori_loop(0, visible, first, jnp.full((rows, 1), -1e30, jnp.float32))

    def second(c, carry):
        totals, acc = carry
        start = pl.multiple_of(c * width, width)
        probs = jnp.exp(s_sc[:, pl.ds(start, width)] - row_max)
        totals = totals + jnp.sum(probs, axis=1, keepdims=True)
        v = gather(v_ref, c)
        acc = acc + jnp.dot(probs.astype(jnp.bfloat16), v, preferred_element_type=jnp.float32)
        return totals, acc

    totals, acc = lax.fori_loop(
        0,
        visible,
        second,
        (jnp.zeros((rows, 1), jnp.float32), jnp.zeros((rows, HEAD), jnp.float32)),
    )
    o_ref[...] = (acc / totals).astype(o_ref.dtype)


def attention(queries, kv_rows, order, chunks, key_bias, tile):
    tok_rows = queries.shape[0]
    tile_rows = tok_rows // 2
    key_count = kv_rows.shape[0]
    head_count = queries.shape[1] // HEAD
    cost = pl.CostEstimate(
        flops=tok_rows * key_count * HEAD * head_count,
        transcendentals=tile_rows * key_count * head_count // 2,
        bytes_accessed=(key_count * 2 * HEAD * 2 + tile_rows * HEAD * 4) * head_count,
    )
    return pl.pallas_call(
        attn_kernel,
        out_shape=jax.ShapeDtypeStruct((tile_rows, head_count * HEAD), jnp.bfloat16),
        grid_spec=pltpu.PrefetchScalarGridSpec(
            num_scalar_prefetch=2,
            grid=(head_count,),
            in_specs=[
                pl.BlockSpec((tile_rows, HEAD), lambda h, o, c: (tile, h)),
                pl.BlockSpec((key_count, HEAD), lambda h, o, c: (0, h)),
                pl.BlockSpec((key_count, HEAD), lambda h, o, c: (0, head_count + h)),
                pl.BlockSpec((None, 1, key_count), lambda h, o, c: (tile, 0, 0)),
            ],
            out_specs=pl.BlockSpec((tile_rows, HEAD), lambda h, o, c: (0, h)),
            scratch_shapes=[pltpu.VMEM((tile_rows, key_count), jnp.float32)],
        ),
        compiler_params=pltpu.CompilerParams(vmem_limit_bytes=56 * 1024 * 1024),
        cost_estimate=cost,
    )(order, chunks[tile:tile + 1], queries, kv_rows, kv_rows, key_bias)


def local(queries, keys, values, resid, out_weight, gain, pair_of_device, frame_of_tile):
    tok_rows, row_width = queries.shape
    head_count = row_width // HEAD
    span_rows = tok_rows // 2
    seq_count = lax.axis_size("seq")
    seq_index = lax.axis_index("seq")
    slot_frame = slot_frames(pair_of_device, frame_of_tile, 2 * seq_count)
    own_frames = lax.dynamic_slice_in_dim(slot_frame, 2 * seq_index, 2, 0).astype(jnp.int32)
    slot_count = slot_frame.shape[0]
    slot_ids = jnp.arange(slot_count, dtype=jnp.int32)
    earlier = (slot_frame[None, :] < slot_frame[:, None]) | (
        (slot_frame[None, :] == slot_frame[:, None]) & (slot_ids[None, :] < slot_ids[:, None])
    )
    rank = jnp.sum(earlier.astype(jnp.int32), axis=1)
    order = jnp.sum(
        jnp.where(rank[:, None] == slot_ids[None, :], slot_ids[:, None], 0), axis=0
    ).astype(jnp.int32)
    sorted_frame = jnp.sum(
        jnp.where(rank[:, None] == slot_ids[None, :], slot_frame[:, None], 0), axis=0
    )
    visible = jnp.sum((slot_frame[None, :] <= own_frames[:, None]).astype(jnp.int32), axis=1)
    chunks = ((visible + SLOTS_PER_CHUNK - 1) // SLOTS_PER_CHUNK).astype(jnp.int32)
    key_frame = jnp.repeat(sorted_frame.astype(jnp.int32), span_rows)
    key_bias = jnp.where(
        key_frame[None, :] <= own_frames[:, None], jnp.float32(0.0), jnp.float32(-1e30)
    ).reshape(2, 1, -1)

    kv_local = jnp.concatenate([keys, values], axis=1)
    kv_rows = lax.all_gather(kv_local, "seq", axis=0, tiled=True)
    tp_count = lax.axis_size("tp")
    tp_index = lax.axis_index("tp")
    share_rows = tok_rows // tp_count
    owners = tp_count // 2
    total = jnp.zeros((share_rows, out_weight.shape[1]), jnp.float32)
    for tile in range(2):
        attn = attention(queries, kv_rows, order, chunks, key_bias, tile)
        part = jnp.dot(attn, out_weight, preferred_element_type=jnp.float32).astype(jnp.bfloat16)
        base = tile * owners
        mine = lax.dynamic_slice_in_dim(part, (tp_index % owners) * share_rows, share_rows, 0)
        own = (tp_index // owners) == tile
        total = total + jnp.where(own, mine.astype(jnp.float32), jnp.float32(0.0))
        for shift in range(1, tp_count):
            pairs = [
                (src, (src + shift) % tp_count)
                for src in range(tp_count)
                if base <= (src + shift) % tp_count < base + owners
            ]
            dest = (tp_index + shift) % tp_count
            share = lax.dynamic_slice_in_dim(part, (dest % owners) * share_rows, share_rows, 0)
            got = lax.ppermute(share, "tp", pairs)
            total = total + got.astype(jnp.float32)
    branch = total
    rms = jnp.sqrt(jnp.mean(branch * branch, axis=-1) + 1e-06)
    layer_out = resid.astype(jnp.float32) + gain[None, :] * branch / rms[:, None]
    return layer_out.astype(jnp.bfloat16)


def solution(mesh):
    in_specs = (
        P("seq", "tp"),
        P("seq", "tp"),
        P("seq", "tp"),
        P(("seq", "tp"), None),
        P("tp", None),
        P(),
        P(),
        P(),
    )
    out_specs = P(("seq", "tp"), None)
    return jax.shard_map(local, mesh=mesh, in_specs=in_specs, out_specs=out_specs, check_vma=False)
```

```python
import functools
import math

import jax
import jax.numpy as jnp
from jax import lax
from jax.experimental import pallas as pl
from jax.experimental.pallas import tpu as pltpu
from jax.sharding import PartitionSpec as P

HEAD = 128
SLOTS_PER_CHUNK = 4


def slot_frames(pair_of_device, frame_of_tile, tile_count):
    slot_ids = jnp.arange(tile_count, dtype=jnp.int32)
    paired = jnp.repeat(pair_of_device, 2)
    tile_ids = jnp.where(slot_ids % 2 == 0, paired, tile_count - 1 - paired)
    matches = tile_ids[:, None] == jnp.arange(tile_count, dtype=jnp.int32)[None, :]
    return jnp.sum(jnp.where(matches, frame_of_tile[None, :], 0), axis=1)


def attn_kernel(order_ref, chunks_ref, q_ref, k_ref, v_ref, kb_ref, o_ref, s_sc):
    tile = pl.program_id(1)
    visible = chunks_ref[tile]
    rows = q_ref.shape[0]
    span = k_ref.shape[0] // order_ref.shape[0]
    width = span * SLOTS_PER_CHUNK
    score_scale = 1.0 / math.sqrt(HEAD)
    q = q_ref[...]

    def gather(ref, c):
        pieces = []
        for m in range(SLOTS_PER_CHUNK):
            slot = order_ref[c * SLOTS_PER_CHUNK + m]
            pieces.append(ref[pl.ds(pl.multiple_of(slot * span, span), span), :])
        return jnp.concatenate(pieces, axis=0)

    def first(c, run_max):
        start = pl.multiple_of(c * width, width)
        k = gather(k_ref, c)
        s = lax.dot_general(
            q, k, (((1,), (1,)), ((), ())), preferred_element_type=jnp.float32
        ) * score_scale
        masked = s + kb_ref[:, pl.ds(start, width)]
        s_sc[:, pl.ds(start, width)] = masked
        return jnp.maximum(run_max, jnp.max(masked, axis=1, keepdims=True))

    row_max = lax.fori_loop(0, visible, first, jnp.full((rows, 1), -1e30, jnp.float32))

    def second(c, carry):
        totals, acc = carry
        start = pl.multiple_of(c * width, width)
        probs = jnp.exp(s_sc[:, pl.ds(start, width)] - row_max)
        totals = totals + jnp.sum(probs, axis=1, keepdims=True)
        v = gather(v_ref, c)
        acc = acc + jnp.dot(probs.astype(jnp.bfloat16), v, preferred_element_type=jnp.float32)
        return totals, acc

    totals, acc = lax.fori_loop(
        0,
        visible,
        second,
        (jnp.zeros((rows, 1), jnp.float32), jnp.zeros((rows, HEAD), jnp.float32)),
    )
    o_ref[...] = (acc / totals).astype(o_ref.dtype)


def attention(queries, kv_rows, order, chunks, key_bias):
    tok_rows = queries.shape[0]
    tile_rows = tok_rows // 2
    key_count = kv_rows.shape[0]
    head_count = queries.shape[1] // HEAD
    cost = pl.CostEstimate(
        flops=2 * tok_rows * key_count * HEAD * head_count,
        transcendentals=tok_rows * key_count * head_count // 2,
        bytes_accessed=(key_count * 2 * HEAD * 2 + tok_rows * HEAD * 4) * head_count,
    )
    return pl.pallas_call(
        attn_kernel,
        out_shape=jax.ShapeDtypeStruct((tok_rows, head_count * HEAD), jnp.bfloat16),
        grid_spec=pltpu.PrefetchScalarGridSpec(
            num_scalar_prefetch=2,
            grid=(head_count, 2),
            in_specs=[
                pl.BlockSpec((tile_rows, HEAD), lambda h, i, o, c: (i, h)),
                pl.BlockSpec((key_count, HEAD), lambda h, i, o, c: (0, h)),
                pl.BlockSpec((key_count, HEAD), lambda h, i, o, c: (0, head_count + h)),
                pl.BlockSpec((None, 1, key_count), lambda h, i, o, c: (i, 0, 0)),
            ],
            out_specs=pl.BlockSpec((tile_rows, HEAD), lambda h, i, o, c: (i, h)),
            scratch_shapes=[pltpu.VMEM((tile_rows, key_count), jnp.float32)],
        ),
        compiler_params=pltpu.CompilerParams(vmem_limit_bytes=56 * 1024 * 1024),
        cost_estimate=cost,
    )(order, chunks, queries, kv_rows, kv_rows, key_bias)


def local(queries, keys, values, resid, out_weight, gain, pair_of_device, frame_of_tile):
    tok_rows, row_width = queries.shape
    head_count = row_width // HEAD
    span_rows = tok_rows // 2
    seq_count = lax.axis_size("seq")
    seq_index = lax.axis_index("seq")
    slot_frame = slot_frames(pair_of_device, frame_of_tile, 2 * seq_count)
    own_frames = lax.dynamic_slice_in_dim(slot_frame, 2 * seq_index, 2, 0).astype(jnp.int32)
    slot_count = slot_frame.shape[0]
    slot_ids = jnp.arange(slot_count, dtype=jnp.int32)
    earlier = (slot_frame[None, :] < slot_frame[:, None]) | (
        (slot_frame[None, :] == slot_frame[:, None]) & (slot_ids[None, :] < slot_ids[:, None])
    )
    rank = jnp.sum(earlier.astype(jnp.int32), axis=1)
    order = jnp.sum(
        jnp.where(rank[:, None] == slot_ids[None, :], slot_ids[:, None], 0), axis=0
    ).astype(jnp.int32)
    sorted_frame = jnp.sum(
        jnp.where(rank[:, None] == slot_ids[None, :], slot_frame[:, None], 0), axis=0
    )
    visible = jnp.sum((slot_frame[None, :] <= own_frames[:, None]).astype(jnp.int32), axis=1)
    chunks = ((visible + SLOTS_PER_CHUNK - 1) // SLOTS_PER_CHUNK).astype(jnp.int32)
    key_frame = jnp.repeat(sorted_frame.astype(jnp.int32), span_rows)
    key_bias = jnp.where(
        key_frame[None, :] <= own_frames[:, None], jnp.float32(0.0), jnp.float32(-1e30)
    ).reshape(2, 1, -1)

    kv_local = jnp.concatenate([keys, values], axis=1)
    kv_rows = lax.all_gather(kv_local, "seq", axis=0, tiled=True)
    attn = attention(queries, kv_rows, order, chunks, key_bias)
    partial = jnp.dot(attn, out_weight, preferred_element_type=jnp.float32)

    tp_count = lax.axis_size("tp")
    shares = lax.all_to_all(
        partial.astype(jnp.bfloat16).reshape(tp_count, tok_rows // tp_count, -1),
        "tp",
        0,
        0,
        tiled=False,
    )
    branch = jnp.sum(shares.astype(jnp.float32), axis=0)
    rms = jnp.sqrt(jnp.mean(branch * branch, axis=-1) + 1e-06)
    layer_out = resid.astype(jnp.float32) + gain[None, :] * branch / rms[:, None]
    return layer_out.astype(jnp.bfloat16)


def solution(mesh):
    in_specs = (
        P("seq", "tp"),
        P("seq", "tp"),
        P("seq", "tp"),
        P(("seq", "tp"), None),
        P("tp", None),
        P(),
        P(),
        P(),
    )
    out_specs = P(("seq", "tp"), None)
    return jax.shard_map(local, mesh=mesh, in_specs=in_specs, out_specs=out_specs, check_vma=False)
```

```python
import functools
import math

import jax
import jax.numpy as jnp
from jax import lax
from jax.experimental import pallas as pl
from jax.experimental.pallas import tpu as pltpu
from jax.sharding import PartitionSpec as P

HEAD = 128
SLOTS_PER_CHUNK = 16


def slot_frames(pair_of_device, frame_of_tile, tile_count):
    slot_ids = jnp.arange(tile_count, dtype=jnp.int32)
    paired = jnp.repeat(pair_of_device, 2)
    tile_ids = jnp.where(slot_ids % 2 == 0, paired, tile_count - 1 - paired)
    matches = tile_ids[:, None] == jnp.arange(tile_count, dtype=jnp.int32)[None, :]
    return jnp.sum(jnp.where(matches, frame_of_tile[None, :], 0), axis=1)


def attn_kernel(order_ref, chunks_ref, q_ref, k_ref, v_ref, kb_ref, o_ref, s_sc):
    tile = pl.program_id(1)
    visible = chunks_ref[tile]
    rows = q_ref.shape[0]
    span = k_ref.shape[0] // order_ref.shape[0]
    width = span * SLOTS_PER_CHUNK
    score_scale = 1.0 / math.sqrt(HEAD)
    q = q_ref[...]

    def gather(ref, c):
        pieces = []
        for m in range(SLOTS_PER_CHUNK):
            slot = order_ref[c * SLOTS_PER_CHUNK + m]
            pieces.append(ref[pl.ds(pl.multiple_of(slot * span, span), span), :])
        return jnp.concatenate(pieces, axis=0)

    def first(c, run_max):
        start = pl.multiple_of(c * width, width)
        k = gather(k_ref, c)
        s = lax.dot_general(
            q, k, (((1,), (1,)), ((), ())), preferred_element_type=jnp.float32
        ) * score_scale
        masked = s + kb_ref[:, pl.ds(start, width)]
        s_sc[:, pl.ds(start, width)] = masked
        return jnp.maximum(run_max, jnp.max(masked, axis=1, keepdims=True))

    row_max = lax.fori_loop(0, visible, first, jnp.full((rows, 1), -1e30, jnp.float32))

    def second(c, carry):
        totals, acc = carry
        start = pl.multiple_of(c * width, width)
        probs = jnp.exp(s_sc[:, pl.ds(start, width)] - row_max)
        totals = totals + jnp.sum(probs, axis=1, keepdims=True)
        v = gather(v_ref, c)
        acc = acc + jnp.dot(probs.astype(jnp.bfloat16), v, preferred_element_type=jnp.float32)
        return totals, acc

    totals, acc = lax.fori_loop(
        0,
        visible,
        second,
        (jnp.zeros((rows, 1), jnp.float32), jnp.zeros((rows, HEAD), jnp.float32)),
    )
    o_ref[...] = (acc / totals).astype(o_ref.dtype)


def attention(queries, kv_rows, order, chunks, key_bias):
    tok_rows = queries.shape[0]
    tile_rows = tok_rows // 2
    key_count = kv_rows.shape[0]
    head_count = queries.shape[1] // HEAD
    cost = pl.CostEstimate(
        flops=2 * tok_rows * key_count * HEAD * head_count,
        transcendentals=tok_rows * key_count * head_count // 2,
        bytes_accessed=(key_count * 2 * HEAD * 2 + tok_rows * HEAD * 4) * head_count,
    )
    return pl.pallas_call(
        attn_kernel,
        out_shape=jax.ShapeDtypeStruct((tok_rows, head_count * HEAD), jnp.bfloat16),
        grid_spec=pltpu.PrefetchScalarGridSpec(
            num_scalar_prefetch=2,
            grid=(head_count, 2),
            in_specs=[
                pl.BlockSpec((tile_rows, HEAD), lambda h, i, o, c: (i, h)),
                pl.BlockSpec((key_count, HEAD), lambda h, i, o, c: (0, h)),
                pl.BlockSpec((key_count, HEAD), lambda h, i, o, c: (0, head_count + h)),
                pl.BlockSpec((None, 1, key_count), lambda h, i, o, c: (i, 0, 0)),
            ],
            out_specs=pl.BlockSpec((tile_rows, HEAD), lambda h, i, o, c: (i, h)),
            scratch_shapes=[pltpu.VMEM((tile_rows, key_count), jnp.float32)],
        ),
        compiler_params=pltpu.CompilerParams(vmem_limit_bytes=56 * 1024 * 1024),
        cost_estimate=cost,
    )(order, chunks, queries, kv_rows, kv_rows, key_bias)


def local(queries, keys, values, resid, out_weight, gain, pair_of_device, frame_of_tile):
    tok_rows, row_width = queries.shape
    head_count = row_width // HEAD
    span_rows = tok_rows // 2
    seq_count = lax.axis_size("seq")
    seq_index = lax.axis_index("seq")
    slot_frame = slot_frames(pair_of_device, frame_of_tile, 2 * seq_count)
    own_frames = lax.dynamic_slice_in_dim(slot_frame, 2 * seq_index, 2, 0).astype(jnp.int32)
    slot_count = slot_frame.shape[0]
    slot_ids = jnp.arange(slot_count, dtype=jnp.int32)
    earlier = (slot_frame[None, :] < slot_frame[:, None]) | (
        (slot_frame[None, :] == slot_frame[:, None]) & (slot_ids[None, :] < slot_ids[:, None])
    )
    rank = jnp.sum(earlier.astype(jnp.int32), axis=1)
    order = jnp.sum(
        jnp.where(rank[:, None] == slot_ids[None, :], slot_ids[:, None], 0), axis=0
    ).astype(jnp.int32)
    sorted_frame = jnp.sum(
        jnp.where(rank[:, None] == slot_ids[None, :], slot_frame[:, None], 0), axis=0
    )
    visible = jnp.sum((slot_frame[None, :] <= own_frames[:, None]).astype(jnp.int32), axis=1)
    chunks = ((visible + SLOTS_PER_CHUNK - 1) // SLOTS_PER_CHUNK).astype(jnp.int32)
    key_frame = jnp.repeat(sorted_frame.astype(jnp.int32), span_rows)
    key_bias = jnp.where(
        key_frame[None, :] <= own_frames[:, None], jnp.float32(0.0), jnp.float32(-1e30)
    ).reshape(2, 1, -1)

    kv_local = jnp.concatenate([keys, values], axis=1)
    kv_rows = lax.all_gather(kv_local, "seq", axis=0, tiled=True)
    attn = attention(queries, kv_rows, order, chunks, key_bias)
    partial = jnp.dot(attn, out_weight, preferred_element_type=jnp.float32)

    tp_count = lax.axis_size("tp")
    shares = lax.all_to_all(
        partial.astype(jnp.bfloat16).reshape(tp_count, tok_rows // tp_count, -1),
        "tp",
        0,
        0,
        tiled=False,
    )
    branch = jnp.sum(shares.astype(jnp.float32), axis=0)
    rms = jnp.sqrt(jnp.mean(branch * branch, axis=-1) + 1e-06)
    layer_out = resid.astype(jnp.float32) + gain[None, :] * branch / rms[:, None]
    return layer_out.astype(jnp.bfloat16)


def solution(mesh):
    in_specs = (
        P("seq", "tp"),
        P("seq", "tp"),
        P("seq", "tp"),
        P(("seq", "tp"), None),
        P("tp", None),
        P(),
        P(),
        P(),
    )
    out_specs = P(("seq", "tp"), None)
    return jax.shard_map(local, mesh=mesh, in_specs=in_specs, out_specs=out_specs, check_vma=False)
```

```python
import functools
import math

import jax
import jax.numpy as jnp
from jax import lax
from jax.experimental import pallas as pl
from jax.experimental.pallas import tpu as pltpu
from jax.sharding import PartitionSpec as P

HEAD = 128
SLOTS_PER_CHUNK = 16


def slot_frames(pair_of_device, frame_of_tile, tile_count):
    slot_ids = jnp.arange(tile_count, dtype=jnp.int32)
    paired = jnp.repeat(pair_of_device, 2)
    tile_ids = jnp.where(slot_ids % 2 == 0, paired, tile_count - 1 - paired)
    matches = tile_ids[:, None] == jnp.arange(tile_count, dtype=jnp.int32)[None, :]
    return jnp.sum(jnp.where(matches, frame_of_tile[None, :], 0), axis=1)


def attn_kernel(order_ref, chunks_ref, q_ref, k_ref, v_ref, kb_ref, o_ref):
    tile = pl.program_id(1)
    visible = chunks_ref[tile]
    rows = q_ref.shape[0]
    span = k_ref.shape[0] // order_ref.shape[0]
    width = span * SLOTS_PER_CHUNK
    score_scale = 1.0 / math.sqrt(HEAD)
    q = q_ref[...]

    def gather(ref, c):
        pieces = []
        for m in range(SLOTS_PER_CHUNK):
            slot = order_ref[c * SLOTS_PER_CHUNK + m]
            pieces.append(ref[pl.ds(pl.multiple_of(slot * span, span), span), :])
        return jnp.concatenate(pieces, axis=0)

    def step(c, carry):
        run_max, totals, acc = carry
        start = pl.multiple_of(c * width, width)
        k = gather(k_ref, c)
        s = lax.dot_general(
            q, k, (((1,), (1,)), ((), ())), preferred_element_type=jnp.float32
        ) * score_scale
        masked = s + kb_ref[:, pl.ds(start, width)]
        new_max = jnp.maximum(run_max, jnp.max(masked, axis=1, keepdims=True))
        rescale = jnp.exp(run_max - new_max)
        probs = jnp.exp(masked - new_max)
        totals = totals * rescale + jnp.sum(probs, axis=1, keepdims=True)
        v = gather(v_ref, c)
        acc = acc * rescale + jnp.dot(
            probs.astype(jnp.bfloat16), v, preferred_element_type=jnp.float32
        )
        return new_max, totals, acc

    row_max, totals, acc = lax.fori_loop(
        0,
        visible,
        step,
        (
            jnp.full((rows, 1), -1e30, jnp.float32),
            jnp.zeros((rows, 1), jnp.float32),
            jnp.zeros((rows, HEAD), jnp.float32),
        ),
    )
    o_ref[...] = (acc / totals).astype(o_ref.dtype)


def attention(queries, kv_rows, order, chunks, key_bias):
    tok_rows = queries.shape[0]
    tile_rows = tok_rows // 2
    key_count = kv_rows.shape[0]
    head_count = queries.shape[1] // HEAD
    cost = pl.CostEstimate(
        flops=2 * tok_rows * key_count * HEAD * head_count,
        transcendentals=tok_rows * key_count * head_count // 2,
        bytes_accessed=(key_count * 2 * HEAD * 2 + tok_rows * HEAD * 4) * head_count,
    )
    return pl.pallas_call(
        attn_kernel,
        out_shape=jax.ShapeDtypeStruct((tok_rows, head_count * HEAD), jnp.bfloat16),
        grid_spec=pltpu.PrefetchScalarGridSpec(
            num_scalar_prefetch=2,
            grid=(head_count, 2),
            in_specs=[
                pl.BlockSpec((tile_rows, HEAD), lambda h, i, o, c: (i, h)),
                pl.BlockSpec((key_count, HEAD), lambda h, i, o, c: (0, h)),
                pl.BlockSpec((key_count, HEAD), lambda h, i, o, c: (0, head_count + h)),
                pl.BlockSpec((None, 1, key_count), lambda h, i, o, c: (i, 0, 0)),
            ],
            out_specs=pl.BlockSpec((tile_rows, HEAD), lambda h, i, o, c: (i, h)),
        ),
        compiler_params=pltpu.CompilerParams(vmem_limit_bytes=56 * 1024 * 1024),
        cost_estimate=cost,
    )(order, chunks, queries, kv_rows, kv_rows, key_bias)


def local(queries, keys, values, resid, out_weight, gain, pair_of_device, frame_of_tile):
    tok_rows, row_width = queries.shape
    head_count = row_width // HEAD
    span_rows = tok_rows // 2
    seq_count = lax.axis_size("seq")
    seq_index = lax.axis_index("seq")
    slot_frame = slot_frames(pair_of_device, frame_of_tile, 2 * seq_count)
    own_frames = lax.dynamic_slice_in_dim(slot_frame, 2 * seq_index, 2, 0).astype(jnp.int32)
    slot_count = slot_frame.shape[0]
    slot_ids = jnp.arange(slot_count, dtype=jnp.int32)
    earlier = (slot_frame[None, :] < slot_frame[:, None]) | (
        (slot_frame[None, :] == slot_frame[:, None]) & (slot_ids[None, :] < slot_ids[:, None])
    )
    rank = jnp.sum(earlier.astype(jnp.int32), axis=1)
    order = jnp.sum(
        jnp.where(rank[:, None] == slot_ids[None, :], slot_ids[:, None], 0), axis=0
    ).astype(jnp.int32)
    sorted_frame = jnp.sum(
        jnp.where(rank[:, None] == slot_ids[None, :], slot_frame[:, None], 0), axis=0
    )
    visible = jnp.sum((slot_frame[None, :] <= own_frames[:, None]).astype(jnp.int32), axis=1)
    chunks = ((visible + SLOTS_PER_CHUNK - 1) // SLOTS_PER_CHUNK).astype(jnp.int32)
    key_frame = jnp.repeat(sorted_frame.astype(jnp.int32), span_rows)
    key_bias = jnp.where(
        key_frame[None, :] <= own_frames[:, None], jnp.float32(0.0), jnp.float32(-1e30)
    ).reshape(2, 1, -1)

    kv_local = jnp.concatenate([keys, values], axis=1)
    kv_rows = lax.all_gather(kv_local, "seq", axis=0, tiled=True)
    attn = attention(queries, kv_rows, order, chunks, key_bias)
    partial = jnp.dot(attn, out_weight, preferred_element_type=jnp.float32)

    tp_count = lax.axis_size("tp")
    shares = lax.all_to_all(
        partial.astype(jnp.bfloat16).reshape(tp_count, tok_rows // tp_count, -1),
        "tp",
        0,
        0,
        tiled=False,
    )
    branch = jnp.sum(shares.astype(jnp.float32), axis=0)
    rms = jnp.sqrt(jnp.mean(branch * branch, axis=-1) + 1e-06)
    layer_out = resid.astype(jnp.float32) + gain[None, :] * branch / rms[:, None]
    return layer_out.astype(jnp.bfloat16)


def solution(mesh):
    in_specs = (
        P("seq", "tp"),
        P("seq", "tp"),
        P("seq", "tp"),
        P(("seq", "tp"), None),
        P("tp", None),
        P(),
        P(),
        P(),
    )
    out_specs = P(("seq", "tp"), None)
    return jax.shard_map(local, mesh=mesh, in_specs=in_specs, out_specs=out_specs, check_vma=False)
```

```python
import functools
import math

import jax
import jax.numpy as jnp
from jax import lax
from jax.experimental import pallas as pl
from jax.experimental.pallas import tpu as pltpu
from jax.sharding import PartitionSpec as P

HEAD = 128
SLOTS_PER_CHUNK = 16
GATHER_PIECE_COLS = 32


def slot_frames(pair_of_device, frame_of_tile, tile_count):
    slot_ids = jnp.arange(tile_count, dtype=jnp.int32)
    paired = jnp.repeat(pair_of_device, 2)
    tile_ids = jnp.where(slot_ids % 2 == 0, paired, tile_count - 1 - paired)
    matches = tile_ids[:, None] == jnp.arange(tile_count, dtype=jnp.int32)[None, :]
    return jnp.sum(jnp.where(matches, frame_of_tile[None, :], 0), axis=1)


def attn_kernel(order_ref, chunks_ref, q_ref, k_ref, v_ref, kb_ref, o_ref, s_sc):
    tile = pl.program_id(1)
    visible = chunks_ref[tile]
    rows = q_ref.shape[0]
    span = k_ref.shape[0] // order_ref.shape[0]
    width = span * SLOTS_PER_CHUNK
    score_scale = 1.0 / math.sqrt(HEAD)
    q = q_ref[...]

    def gather(ref, c):
        pieces = []
        for m in range(SLOTS_PER_CHUNK):
            slot = order_ref[c * SLOTS_PER_CHUNK + m]
            pieces.append(ref[pl.ds(pl.multiple_of(slot * span, span), span), :])
        return jnp.concatenate(pieces, axis=0)

    def first(c, run_max):
        start = pl.multiple_of(c * width, width)
        k = gather(k_ref, c)
        s = lax.dot_general(
            q, k, (((1,), (1,)), ((), ())), preferred_element_type=jnp.float32
        ) * score_scale
        masked = s + kb_ref[:, pl.ds(start, width)]
        s_sc[:, pl.ds(start, width)] = masked
        return jnp.maximum(run_max, jnp.max(masked, axis=1, keepdims=True))

    row_max = lax.fori_loop(0, visible, first, jnp.full((rows, 1), -1e30, jnp.float32))

    def second(c, carry):
        totals, acc = carry
        start = pl.multiple_of(c * width, width)
        probs = jnp.exp(s_sc[:, pl.ds(start, width)] - row_max)
        totals = totals + jnp.sum(probs, axis=1, keepdims=True)
        v = gather(v_ref, c)
        acc = acc + jnp.dot(probs.astype(jnp.bfloat16), v, preferred_element_type=jnp.float32)
        return totals, acc

    totals, acc = lax.fori_loop(
        0,
        visible,
        second,
        (jnp.zeros((rows, 1), jnp.float32), jnp.zeros((rows, HEAD), jnp.float32)),
    )
    o_ref[...] = (acc / totals).astype(o_ref.dtype)


def attention(queries, kv_rows, order, chunks, key_bias):
    tok_rows = queries.shape[0]
    tile_rows = tok_rows // 2
    key_count = kv_rows.shape[0]
    head_count = queries.shape[1] // HEAD
    cost = pl.CostEstimate(
        flops=2 * tok_rows * key_count * HEAD * head_count,
        transcendentals=tok_rows * key_count * head_count // 2,
        bytes_accessed=(key_count * 2 * HEAD * 2 + tok_rows * HEAD * 4) * head_count,
    )
    return pl.pallas_call(
        attn_kernel,
        out_shape=jax.ShapeDtypeStruct((tok_rows, head_count * HEAD), jnp.bfloat16),
        grid_spec=pltpu.PrefetchScalarGridSpec(
            num_scalar_prefetch=2,
            grid=(head_count, 2),
            in_specs=[
                pl.BlockSpec((tile_rows, HEAD), lambda h, i, o, c: (i, h)),
                pl.BlockSpec((key_count, HEAD), lambda h, i, o, c: (0, h)),
                pl.BlockSpec((key_count, HEAD), lambda h, i, o, c: (0, head_count + h)),
                pl.BlockSpec((None, 1, key_count), lambda h, i, o, c: (i, 0, 0)),
            ],
            out_specs=pl.BlockSpec((tile_rows, HEAD), lambda h, i, o, c: (i, h)),
            scratch_shapes=[pltpu.VMEM((tile_rows, key_count), jnp.float32)],
        ),
        compiler_params=pltpu.CompilerParams(vmem_limit_bytes=56 * 1024 * 1024),
        cost_estimate=cost,
    )(order, chunks, queries, kv_rows, kv_rows, key_bias)


def local(queries, keys, values, resid, out_weight, gain, pair_of_device, frame_of_tile):
    tok_rows, row_width = queries.shape
    head_count = row_width // HEAD
    span_rows = tok_rows // 2
    seq_count = lax.axis_size("seq")
    seq_index = lax.axis_index("seq")
    slot_frame = slot_frames(pair_of_device, frame_of_tile, 2 * seq_count)
    own_frames = lax.dynamic_slice_in_dim(slot_frame, 2 * seq_index, 2, 0).astype(jnp.int32)
    slot_count = slot_frame.shape[0]
    slot_ids = jnp.arange(slot_count, dtype=jnp.int32)
    earlier = (slot_frame[None, :] < slot_frame[:, None]) | (
        (slot_frame[None, :] == slot_frame[:, None]) & (slot_ids[None, :] < slot_ids[:, None])
    )
    rank = jnp.sum(earlier.astype(jnp.int32), axis=1)
    order = jnp.sum(
        jnp.where(rank[:, None] == slot_ids[None, :], slot_ids[:, None], 0), axis=0
    ).astype(jnp.int32)
    sorted_frame = jnp.sum(
        jnp.where(rank[:, None] == slot_ids[None, :], slot_frame[:, None], 0), axis=0
    )
    visible = jnp.sum((slot_frame[None, :] <= own_frames[:, None]).astype(jnp.int32), axis=1)
    chunks = ((visible + SLOTS_PER_CHUNK - 1) // SLOTS_PER_CHUNK).astype(jnp.int32)
    key_frame = jnp.repeat(sorted_frame.astype(jnp.int32), span_rows)
    key_bias = jnp.where(
        key_frame[None, :] <= own_frames[:, None], jnp.float32(0.0), jnp.float32(-1e30)
    ).reshape(2, 1, -1)

    kv_local = jnp.concatenate([keys, values], axis=1)
    piece = GATHER_PIECE_COLS
    kv_rows = jnp.concatenate(
        [
            lax.all_gather(kv_local[:, i:i + piece], "seq", axis=0, tiled=True)
            for i in range(0, kv_local.shape[1], piece)
        ],
        axis=1,
    )
    attn = attention(queries, kv_rows, order, chunks, key_bias)
    partial = jnp.dot(attn, out_weight, preferred_element_type=jnp.float32)

    tp_count = lax.axis_size("tp")
    shares = lax.all_to_all(
        partial.astype(jnp.bfloat16).reshape(tp_count, tok_rows // tp_count, -1),
        "tp",
        0,
        0,
        tiled=False,
    )
    branch = jnp.sum(shares.astype(jnp.float32), axis=0)
    rms = jnp.sqrt(jnp.mean(branch * branch, axis=-1) + 1e-06)
    layer_out = resid.astype(jnp.float32) + gain[None, :] * branch / rms[:, None]
    return layer_out.astype(jnp.bfloat16)


def solution(mesh):
    in_specs = (
        P("seq", "tp"),
        P("seq", "tp"),
        P("seq", "tp"),
        P(("seq", "tp"), None),
        P("tp", None),
        P(),
        P(),
        P(),
    )
    out_specs = P(("seq", "tp"), None)
    return jax.shard_map(local, mesh=mesh, in_specs=in_specs, out_specs=out_specs, check_vma=False)
```

```python
import functools
import math

import jax
import jax.numpy as jnp
from jax import lax
from jax.experimental import pallas as pl
from jax.experimental.pallas import tpu as pltpu
from jax.sharding import PartitionSpec as P

HEAD = 128
SLOTS_PER_UNIT = 8


def slot_frames(pair_of_device, frame_of_tile, tile_count):
    slot_ids = jnp.arange(tile_count, dtype=jnp.int32)
    paired = jnp.repeat(pair_of_device, 2)
    tile_ids = jnp.where(slot_ids % 2 == 0, paired, tile_count - 1 - paired)
    matches = tile_ids[:, None] == jnp.arange(tile_count, dtype=jnp.int32)[None, :]
    return jnp.sum(jnp.where(matches, frame_of_tile[None, :], 0), axis=1)


def attn_kernel(order_ref, units_ref, q_ref, k_ref, v_ref, kb_ref, o_ref, s_sc):
    tile = pl.program_id(1)
    units = units_ref[tile]
    pairs = units // 2
    odd = units % 2
    rows = q_ref.shape[0]
    span = k_ref.shape[0] // order_ref.shape[0]
    unit = span * SLOTS_PER_UNIT
    score_scale = 1.0 / math.sqrt(HEAD)
    q = q_ref[...]

    def gather(ref, first, count):
        pieces = []
        for m in range(count):
            slot = order_ref[first + m]
            pieces.append(ref[pl.ds(pl.multiple_of(slot * span, span), span), :])
        return jnp.concatenate(pieces, axis=0)

    def first_pass(start_unit, count, run_max):
        start = pl.multiple_of(start_unit * unit, unit)
        width = count * unit
        k = gather(k_ref, start_unit * SLOTS_PER_UNIT, count * SLOTS_PER_UNIT)
        s = lax.dot_general(
            q, k, (((1,), (1,)), ((), ())), preferred_element_type=jnp.float32
        ) * score_scale
        masked = s + kb_ref[:, pl.ds(start, width)]
        s_sc[:, pl.ds(start, width)] = masked
        return jnp.maximum(run_max, jnp.max(masked, axis=1, keepdims=True))

    row_max = lax.fori_loop(
        0, pairs, lambda c, m: first_pass(2 * c, 2, m), jnp.full((rows, 1), -1e30, jnp.float32)
    )
    row_max = lax.fori_loop(0, odd, lambda c, m: first_pass(2 * pairs, 1, m), row_max)

    def second_pass(start_unit, count, carry):
        totals, acc = carry
        start = pl.multiple_of(start_unit * unit, unit)
        width = count * unit
        probs = jnp.exp(s_sc[:, pl.ds(start, width)] - row_max)
        totals = totals + jnp.sum(probs, axis=1, keepdims=True)
        v = gather(v_ref, start_unit * SLOTS_PER_UNIT, count * SLOTS_PER_UNIT)
        acc = acc + jnp.dot(probs.astype(jnp.bfloat16), v, preferred_element_type=jnp.float32)
        return totals, acc

    carry = lax.fori_loop(
        0,
        pairs,
        lambda c, t: second_pass(2 * c, 2, t),
        (jnp.zeros((rows, 1), jnp.float32), jnp.zeros((rows, HEAD), jnp.float32)),
    )
    totals, acc = lax.fori_loop(0, odd, lambda c, t: second_pass(2 * pairs, 1, t), carry)
    o_ref[...] = (acc / totals).astype(o_ref.dtype)


def attention(queries, kv_rows, order, chunks, key_bias):
    tok_rows = queries.shape[0]
    tile_rows = tok_rows // 2
    key_count = kv_rows.shape[0]
    head_count = queries.shape[1] // HEAD
    cost = pl.CostEstimate(
        flops=2 * tok_rows * key_count * HEAD * head_count,
        transcendentals=tok_rows * key_count * head_count // 2,
        bytes_accessed=(key_count * 2 * HEAD * 2 + tok_rows * HEAD * 4) * head_count,
    )
    return pl.pallas_call(
        attn_kernel,
        out_shape=jax.ShapeDtypeStruct((tok_rows, head_count * HEAD), jnp.bfloat16),
        grid_spec=pltpu.PrefetchScalarGridSpec(
            num_scalar_prefetch=2,
            grid=(head_count, 2),
            in_specs=[
                pl.BlockSpec((tile_rows, HEAD), lambda h, i, o, c: (i, h)),
                pl.BlockSpec((key_count, HEAD), lambda h, i, o, c: (0, h)),
                pl.BlockSpec((key_count, HEAD), lambda h, i, o, c: (0, head_count + h)),
                pl.BlockSpec((None, 1, key_count), lambda h, i, o, c: (i, 0, 0)),
            ],
            out_specs=pl.BlockSpec((tile_rows, HEAD), lambda h, i, o, c: (i, h)),
            scratch_shapes=[pltpu.VMEM((tile_rows, key_count), jnp.float32)],
        ),
        compiler_params=pltpu.CompilerParams(vmem_limit_bytes=56 * 1024 * 1024),
        cost_estimate=cost,
    )(order, chunks, queries, kv_rows, kv_rows, key_bias)


def local(queries, keys, values, resid, out_weight, gain, pair_of_device, frame_of_tile):
    tok_rows, row_width = queries.shape
    head_count = row_width // HEAD
    span_rows = tok_rows // 2
    seq_count = lax.axis_size("seq")
    seq_index = lax.axis_index("seq")
    slot_frame = slot_frames(pair_of_device, frame_of_tile, 2 * seq_count)
    own_frames = lax.dynamic_slice_in_dim(slot_frame, 2 * seq_index, 2, 0).astype(jnp.int32)
    slot_count = slot_frame.shape[0]
    slot_ids = jnp.arange(slot_count, dtype=jnp.int32)
    earlier = (slot_frame[None, :] < slot_frame[:, None]) | (
        (slot_frame[None, :] == slot_frame[:, None]) & (slot_ids[None, :] < slot_ids[:, None])
    )
    rank = jnp.sum(earlier.astype(jnp.int32), axis=1)
    order = jnp.sum(
        jnp.where(rank[:, None] == slot_ids[None, :], slot_ids[:, None], 0), axis=0
    ).astype(jnp.int32)
    sorted_frame = jnp.sum(
        jnp.where(rank[:, None] == slot_ids[None, :], slot_frame[:, None], 0), axis=0
    )
    visible = jnp.sum((slot_frame[None, :] <= own_frames[:, None]).astype(jnp.int32), axis=1)
    chunks = ((visible + SLOTS_PER_UNIT - 1) // SLOTS_PER_UNIT).astype(jnp.int32)
    key_frame = jnp.repeat(sorted_frame.astype(jnp.int32), span_rows)
    key_bias = jnp.where(
        key_frame[None, :] <= own_frames[:, None], jnp.float32(0.0), jnp.float32(-1e30)
    ).reshape(2, 1, -1)

    kv_local = jnp.concatenate([keys, values], axis=1)
    kv_rows = lax.all_gather(kv_local, "seq", axis=0, tiled=True)
    attn = attention(queries, kv_rows, order, chunks, key_bias)
    partial = jnp.dot(attn, out_weight, preferred_element_type=jnp.float32)

    tp_count = lax.axis_size("tp")
    shares = lax.all_to_all(
        partial.astype(jnp.bfloat16).reshape(tp_count, tok_rows // tp_count, -1),
        "tp",
        0,
        0,
        tiled=False,
    )
    branch = jnp.sum(shares.astype(jnp.float32), axis=0)
    rms = jnp.sqrt(jnp.mean(branch * branch, axis=-1) + 1e-06)
    layer_out = resid.astype(jnp.float32) + gain[None, :] * branch / rms[:, None]
    return layer_out.astype(jnp.bfloat16)


def solution(mesh):
    in_specs = (
        P("seq", "tp"),
        P("seq", "tp"),
        P("seq", "tp"),
        P(("seq", "tp"), None),
        P("tp", None),
        P(),
        P(),
        P(),
    )
    out_specs = P(("seq", "tp"), None)
    return jax.shard_map(local, mesh=mesh, in_specs=in_specs, out_specs=out_specs, check_vma=False)
```

```python
import functools
import math

import jax
import jax.numpy as jnp
from jax import lax
from jax.experimental import pallas as pl
from jax.experimental.pallas import tpu as pltpu
from jax.sharding import PartitionSpec as P

HEAD = 128
SLOTS_PER_CHUNK = 16


def slot_frames(pair_of_device, frame_of_tile, tile_count):
    slot_ids = jnp.arange(tile_count, dtype=jnp.int32)
    paired = jnp.repeat(pair_of_device, 2)
    tile_ids = jnp.where(slot_ids % 2 == 0, paired, tile_count - 1 - paired)
    matches = tile_ids[:, None] == jnp.arange(tile_count, dtype=jnp.int32)[None, :]
    return jnp.sum(jnp.where(matches, frame_of_tile[None, :], 0), axis=1)


def attn_kernel(order_ref, chunks_ref, q_ref, kv_ref, kb_ref, o_ref, s_sc):
    tile = pl.program_id(1)
    visible = chunks_ref[tile]
    rows = q_ref.shape[0]
    span = kv_ref.shape[0] // (2 * order_ref.shape[0])
    width = span * SLOTS_PER_CHUNK
    score_scale = 1.0 / math.sqrt(HEAD)
    q = q_ref[...]

    def gather(base, c):
        pieces = []
        for m in range(SLOTS_PER_CHUNK):
            slot = order_ref[c * SLOTS_PER_CHUNK + m]
            row = (slot // 2) * 4 * span + (slot % 2) * span + base
            pieces.append(kv_ref[pl.ds(pl.multiple_of(row, span), span), :])
        return jnp.concatenate(pieces, axis=0)

    def first(c, run_max):
        start = pl.multiple_of(c * width, width)
        k = gather(0, c)
        s = lax.dot_general(
            q, k, (((1,), (1,)), ((), ())), preferred_element_type=jnp.float32
        ) * score_scale
        masked = s + kb_ref[:, pl.ds(start, width)]
        s_sc[:, pl.ds(start, width)] = masked
        return jnp.maximum(run_max, jnp.max(masked, axis=1, keepdims=True))

    row_max = lax.fori_loop(0, visible, first, jnp.full((rows, 1), -1e30, jnp.float32))

    def second(c, carry):
        totals, acc = carry
        start = pl.multiple_of(c * width, width)
        probs = jnp.exp(s_sc[:, pl.ds(start, width)] - row_max)
        totals = totals + jnp.sum(probs, axis=1, keepdims=True)
        v = gather(2 * span, c)
        acc = acc + jnp.dot(probs.astype(jnp.bfloat16), v, preferred_element_type=jnp.float32)
        return totals, acc

    totals, acc = lax.fori_loop(
        0,
        visible,
        second,
        (jnp.zeros((rows, 1), jnp.float32), jnp.zeros((rows, HEAD), jnp.float32)),
    )
    o_ref[...] = (acc / totals).astype(o_ref.dtype)


def attention(queries, kv_rows, order, chunks, key_bias):
    tok_rows = queries.shape[0]
    tile_rows = tok_rows // 2
    key_count = kv_rows.shape[0] // 2
    head_count = queries.shape[1] // HEAD
    cost = pl.CostEstimate(
        flops=2 * tok_rows * key_count * HEAD * head_count,
        transcendentals=tok_rows * key_count * head_count // 2,
        bytes_accessed=(key_count * 2 * HEAD * 2 + tok_rows * HEAD * 4) * head_count,
    )
    return pl.pallas_call(
        attn_kernel,
        out_shape=jax.ShapeDtypeStruct((tok_rows, head_count * HEAD), jnp.bfloat16),
        grid_spec=pltpu.PrefetchScalarGridSpec(
            num_scalar_prefetch=2,
            grid=(head_count, 2),
            in_specs=[
                pl.BlockSpec((tile_rows, HEAD), lambda h, i, o, c: (i, h)),
                pl.BlockSpec((2 * key_count, HEAD), lambda h, i, o, c: (0, h)),
                pl.BlockSpec((None, 1, key_count), lambda h, i, o, c: (i, 0, 0)),
            ],
            out_specs=pl.BlockSpec((tile_rows, HEAD), lambda h, i, o, c: (i, h)),
            scratch_shapes=[pltpu.VMEM((tile_rows, key_count), jnp.float32)],
        ),
        compiler_params=pltpu.CompilerParams(vmem_limit_bytes=56 * 1024 * 1024),
        cost_estimate=cost,
    )(order, chunks, queries, kv_rows, key_bias)


def local(queries, keys, values, resid, out_weight, gain, pair_of_device, frame_of_tile):
    tok_rows, row_width = queries.shape
    head_count = row_width // HEAD
    span_rows = tok_rows // 2
    seq_count = lax.axis_size("seq")
    seq_index = lax.axis_index("seq")
    slot_frame = slot_frames(pair_of_device, frame_of_tile, 2 * seq_count)
    own_frames = lax.dynamic_slice_in_dim(slot_frame, 2 * seq_index, 2, 0).astype(jnp.int32)
    slot_count = slot_frame.shape[0]
    slot_ids = jnp.arange(slot_count, dtype=jnp.int32)
    earlier = (slot_frame[None, :] < slot_frame[:, None]) | (
        (slot_frame[None, :] == slot_frame[:, None]) & (slot_ids[None, :] < slot_ids[:, None])
    )
    rank = jnp.sum(earlier.astype(jnp.int32), axis=1)
    order = jnp.sum(
        jnp.where(rank[:, None] == slot_ids[None, :], slot_ids[:, None], 0), axis=0
    ).astype(jnp.int32)
    sorted_frame = jnp.sum(
        jnp.where(rank[:, None] == slot_ids[None, :], slot_frame[:, None], 0), axis=0
    )
    visible = jnp.sum((slot_frame[None, :] <= own_frames[:, None]).astype(jnp.int32), axis=1)
    chunks = ((visible + SLOTS_PER_CHUNK - 1) // SLOTS_PER_CHUNK).astype(jnp.int32)
    key_frame = jnp.repeat(sorted_frame.astype(jnp.int32), span_rows)
    key_bias = jnp.where(
        key_frame[None, :] <= own_frames[:, None], jnp.float32(0.0), jnp.float32(-1e30)
    ).reshape(2, 1, -1)

    kv_local = jnp.concatenate([keys, values], axis=0)
    kv_rows = lax.all_gather(kv_local, "seq", axis=0, tiled=True)
    attn = attention(queries, kv_rows, order, chunks, key_bias)
    partial = jnp.dot(attn, out_weight, preferred_element_type=jnp.float32)

    tp_count = lax.axis_size("tp")
    shares = lax.all_to_all(
        partial.astype(jnp.bfloat16).reshape(tp_count, tok_rows // tp_count, -1),
        "tp",
        0,
        0,
        tiled=False,
    )
    branch = jnp.sum(shares.astype(jnp.float32), axis=0)
    rms = jnp.sqrt(jnp.mean(branch * branch, axis=-1) + 1e-06)
    layer_out = resid.astype(jnp.float32) + gain[None, :] * branch / rms[:, None]
    return layer_out.astype(jnp.bfloat16)


def solution(mesh):
    in_specs = (
        P("seq", "tp"),
        P("seq", "tp"),
        P("seq", "tp"),
        P(("seq", "tp"), None),
        P("tp", None),
        P(),
        P(),
        P(),
    )
    out_specs = P(("seq", "tp"), None)
    return jax.shard_map(local, mesh=mesh, in_specs=in_specs, out_specs=out_specs, check_vma=False)
```

```python
import functools
import math

import jax
import jax.numpy as jnp
from jax import lax
from jax.experimental import pallas as pl
from jax.experimental.pallas import tpu as pltpu
from jax.sharding import PartitionSpec as P

HEAD = 128
SLOTS_PER_CHUNK = 16


def slot_frames(pair_of_device, frame_of_tile, tile_count):
    slot_ids = jnp.arange(tile_count, dtype=jnp.int32)
    paired = jnp.repeat(pair_of_device, 2)
    tile_ids = jnp.where(slot_ids % 2 == 0, paired, tile_count - 1 - paired)
    matches = tile_ids[:, None] == jnp.arange(tile_count, dtype=jnp.int32)[None, :]
    return jnp.sum(jnp.where(matches, frame_of_tile[None, :], 0), axis=1)


def attn_kernel(order_ref, chunks_ref, q_ref, k_ref, v_ref, kb_ref, o_ref, s_sc):
    tile = pl.program_id(1)
    visible = chunks_ref[tile]
    rows = q_ref.shape[0]
    span = k_ref.shape[0] // order_ref.shape[0]
    width = span * SLOTS_PER_CHUNK
    score_scale = 1.0 / math.sqrt(HEAD)
    q = q_ref[...]

    def gather(ref, c):
        pieces = []
        for m in range(SLOTS_PER_CHUNK):
            slot = order_ref[c * SLOTS_PER_CHUNK + m]
            pieces.append(ref[pl.ds(pl.multiple_of(slot * span, span), span), :])
        return jnp.concatenate(pieces, axis=0)

    def first(c, run_max):
        start = pl.multiple_of(c * width, width)
        k = gather(k_ref, c)
        s = lax.dot_general(
            q, k, (((1,), (1,)), ((), ())), preferred_element_type=jnp.float32
        ) * score_scale
        masked = s + kb_ref[:, pl.ds(start, width)]
        s_sc[:, pl.ds(start, width)] = masked
        return jnp.maximum(run_max, jnp.max(masked, axis=1, keepdims=True))

    row_max = lax.fori_loop(0, visible, first, jnp.full((rows, 1), -1e30, jnp.float32))

    def second(c, carry):
        totals, acc = carry
        start = pl.multiple_of(c * width, width)
        probs = jnp.exp(s_sc[:, pl.ds(start, width)] - row_max)
        totals = totals + jnp.sum(probs, axis=1, keepdims=True)
        v = gather(v_ref, c)
        acc = acc + jnp.dot(probs.astype(jnp.bfloat16), v, preferred_element_type=jnp.float32)
        return totals, acc

    totals, acc = lax.fori_loop(
        0,
        visible,
        second,
        (jnp.zeros((rows, 1), jnp.float32), jnp.zeros((rows, HEAD), jnp.float32)),
    )
    o_ref[...] = (acc / totals).astype(o_ref.dtype)


def attention(queries, kv_rows, order, chunks, key_bias):
    tok_rows = queries.shape[0]
    tile_rows = tok_rows // 2
    key_count = kv_rows.shape[0]
    head_count = queries.shape[1] // HEAD
    cost = pl.CostEstimate(
        flops=2 * tok_rows * key_count * HEAD * head_count,
        transcendentals=tok_rows * key_count * head_count // 2,
        bytes_accessed=(key_count * 2 * HEAD * 2 + tok_rows * HEAD * 4) * head_count,
    )
    return pl.pallas_call(
        attn_kernel,
        out_shape=jax.ShapeDtypeStruct((tok_rows, head_count * HEAD), jnp.bfloat16),
        grid_spec=pltpu.PrefetchScalarGridSpec(
            num_scalar_prefetch=2,
            grid=(head_count, 2),
            in_specs=[
                pl.BlockSpec((tile_rows, HEAD), lambda h, i, o, c: (i, h)),
                pl.BlockSpec((key_count, HEAD), lambda h, i, o, c: (0, h)),
                pl.BlockSpec((key_count, HEAD), lambda h, i, o, c: (0, head_count + h)),
                pl.BlockSpec((None, 1, key_count), lambda h, i, o, c: (i, 0, 0)),
            ],
            out_specs=pl.BlockSpec((tile_rows, HEAD), lambda h, i, o, c: (i, h)),
            scratch_shapes=[pltpu.VMEM((tile_rows, key_count), jnp.float32)],
        ),
        compiler_params=pltpu.CompilerParams(vmem_limit_bytes=56 * 1024 * 1024),
        cost_estimate=cost,
    )(order, chunks, queries, kv_rows, kv_rows, key_bias)


def local(queries, keys, values, resid, out_weight, gain, pair_of_device, frame_of_tile):
    tok_rows, row_width = queries.shape
    head_count = row_width // HEAD
    span_rows = tok_rows // 2
    seq_count = lax.axis_size("seq")
    seq_index = lax.axis_index("seq")
    slot_frame = slot_frames(pair_of_device, frame_of_tile, 2 * seq_count)
    own_frames = lax.dynamic_slice_in_dim(slot_frame, 2 * seq_index, 2, 0).astype(jnp.int32)
    slot_count = slot_frame.shape[0]
    slot_ids = jnp.arange(slot_count, dtype=jnp.int32)
    earlier = (slot_frame[None, :] < slot_frame[:, None]) | (
        (slot_frame[None, :] == slot_frame[:, None]) & (slot_ids[None, :] < slot_ids[:, None])
    )
    rank = jnp.sum(earlier.astype(jnp.int32), axis=1)
    order = jnp.sum(
        jnp.where(rank[:, None] == slot_ids[None, :], slot_ids[:, None], 0), axis=0
    ).astype(jnp.int32)
    sorted_frame = jnp.sum(
        jnp.where(rank[:, None] == slot_ids[None, :], slot_frame[:, None], 0), axis=0
    )
    visible = jnp.sum((slot_frame[None, :] <= own_frames[:, None]).astype(jnp.int32), axis=1)
    chunks = ((visible + SLOTS_PER_CHUNK - 1) // SLOTS_PER_CHUNK).astype(jnp.int32)
    key_frame = jnp.repeat(sorted_frame.astype(jnp.int32), span_rows)
    key_bias = jnp.where(
        key_frame[None, :] <= own_frames[:, None], jnp.float32(0.0), jnp.float32(-1e30)
    ).reshape(2, 1, -1)

    kv_local = jnp.concatenate([keys, values], axis=1)
    kv_rows = lax.all_gather(kv_local, "seq", axis=0, tiled=True)
    attn = attention(queries, kv_rows, order, chunks, key_bias)
    tp_count = lax.axis_size("tp")
    share_rows = tok_rows // tp_count
    split = out_weight.shape[1] // 4
    part_a = jnp.dot(attn, out_weight[:, :split], preferred_element_type=jnp.float32)
    branch_a = lax.psum_scatter(
        part_a.astype(jnp.bfloat16), "tp", scatter_dimension=0, tiled=True
    ).astype(jnp.float32)
    part_b = jnp.dot(attn, out_weight[:, split:], preferred_element_type=jnp.float32)
    shares = lax.all_to_all(
        part_b.astype(jnp.bfloat16).reshape(tp_count, share_rows, -1), "tp", 0, 0, tiled=False
    )
    branch_b = jnp.sum(shares.astype(jnp.float32), axis=0)
    branch = jnp.concatenate([branch_a, branch_b], axis=1)
    rms = jnp.sqrt(jnp.mean(branch * branch, axis=-1) + 1e-06)
    layer_out = resid.astype(jnp.float32) + gain[None, :] * branch / rms[:, None]
    return layer_out.astype(jnp.bfloat16)


def solution(mesh):
    in_specs = (
        P("seq", "tp"),
        P("seq", "tp"),
        P("seq", "tp"),
        P(("seq", "tp"), None),
        P("tp", None),
        P(),
        P(),
        P(),
    )
    out_specs = P(("seq", "tp"), None)
    return jax.shard_map(local, mesh=mesh, in_specs=in_specs, out_specs=out_specs, check_vma=False)
```

```python
import functools
import math

import jax
import jax.numpy as jnp
from jax import lax
from jax.experimental import pallas as pl
from jax.experimental.pallas import tpu as pltpu
from jax.sharding import PartitionSpec as P

HEAD = 128
SLOTS_PER_CHUNK = 16
PROJ_BLOCKS = 8


def slot_frames(pair_of_device, frame_of_tile, tile_count):
    slot_ids = jnp.arange(tile_count, dtype=jnp.int32)
    paired = jnp.repeat(pair_of_device, 2)
    tile_ids = jnp.where(slot_ids % 2 == 0, paired, tile_count - 1 - paired)
    matches = tile_ids[:, None] == jnp.arange(tile_count, dtype=jnp.int32)[None, :]
    return jnp.sum(jnp.where(matches, frame_of_tile[None, :], 0), axis=1)


def attn_kernel(order_ref, chunks_ref, q_ref, k_ref, v_ref, kb_ref, w_ref, o_ref, s_sc, a_sc):
    tile = pl.program_id(1)
    visible = chunks_ref[tile]
    rows = q_ref.shape[0]
    span = k_ref.shape[0] // order_ref.shape[0]
    width = span * SLOTS_PER_CHUNK
    score_scale = 1.0 / math.sqrt(HEAD)
    q = q_ref[...]

    def gather(ref, c):
        pieces = []
        for m in range(SLOTS_PER_CHUNK):
            slot = order_ref[c * SLOTS_PER_CHUNK + m]
            pieces.append(ref[pl.ds(pl.multiple_of(slot * span, span), span), :])
        return jnp.concatenate(pieces, axis=0)

    def first(c, run_max):
        start = pl.multiple_of(c * width, width)
        k = gather(k_ref, c)
        s = lax.dot_general(
            q, k, (((1,), (1,)), ((), ())), preferred_element_type=jnp.float32
        ) * score_scale
        masked = s + kb_ref[:, pl.ds(start, width)]
        s_sc[:, pl.ds(start, width)] = masked
        return jnp.maximum(run_max, jnp.max(masked, axis=1, keepdims=True))

    row_max = lax.fori_loop(0, visible, first, jnp.full((rows, 1), -1e30, jnp.float32))

    def second(c, carry):
        totals, acc = carry
        start = pl.multiple_of(c * width, width)
        probs = jnp.exp(s_sc[:, pl.ds(start, width)] - row_max)
        totals = totals + jnp.sum(probs, axis=1, keepdims=True)
        v = gather(v_ref, c)
        acc = acc + jnp.dot(probs.astype(jnp.bfloat16), v, preferred_element_type=jnp.float32)
        return totals, acc

    totals, acc = lax.fori_loop(
        0,
        visible,
        second,
        (jnp.zeros((rows, 1), jnp.float32), jnp.zeros((rows, HEAD), jnp.float32)),
    )
    head = pl.program_id(0)
    a_sc[tile, :, pl.ds(pl.multiple_of(head * HEAD, HEAD), HEAD)] = (acc / totals).astype(a_sc.dtype)

    @pl.when(head == pl.num_programs(0) - 1)
    def _():
        attn = a_sc[tile]
        cols = w_ref.shape[1] // PROJ_BLOCKS
        for j in range(PROJ_BLOCKS):
            o_ref[:, j * cols:(j + 1) * cols] = jnp.dot(
                attn, w_ref[:, j * cols:(j + 1) * cols], preferred_element_type=jnp.float32
            ).astype(o_ref.dtype)


def attention(queries, kv_rows, order, chunks, key_bias, out_weight):
    tok_rows = queries.shape[0]
    tile_rows = tok_rows // 2
    key_count = kv_rows.shape[0]
    head_count = queries.shape[1] // HEAD
    cost = pl.CostEstimate(
        flops=2 * tok_rows * key_count * HEAD * head_count
        + 2 * tok_rows * out_weight.shape[0] * out_weight.shape[1],
        transcendentals=tok_rows * key_count * head_count // 2,
        bytes_accessed=(key_count * 2 * HEAD * 2 + tok_rows * HEAD * 4) * head_count,
    )
    return pl.pallas_call(
        attn_kernel,
        out_shape=jax.ShapeDtypeStruct((tok_rows, out_weight.shape[1]), jnp.bfloat16),
        grid_spec=pltpu.PrefetchScalarGridSpec(
            num_scalar_prefetch=2,
            grid=(head_count, 2),
            in_specs=[
                pl.BlockSpec((tile_rows, HEAD), lambda h, i, o, c: (i, h)),
                pl.BlockSpec((key_count, HEAD), lambda h, i, o, c: (0, h)),
                pl.BlockSpec((key_count, HEAD), lambda h, i, o, c: (0, head_count + h)),
                pl.BlockSpec((None, 1, key_count), lambda h, i, o, c: (i, 0, 0)),
                pl.BlockSpec(out_weight.shape, lambda h, i, o, c: (0, 0)),
            ],
            out_specs=pl.BlockSpec((tile_rows, out_weight.shape[1]), lambda h, i, o, c: (i, 0)),
            scratch_shapes=[
                pltpu.VMEM((tile_rows, key_count), jnp.float32),
                pltpu.VMEM((2, tile_rows, head_count * HEAD), jnp.bfloat16),
            ],
        ),
        compiler_params=pltpu.CompilerParams(vmem_limit_bytes=56 * 1024 * 1024),
        cost_estimate=cost,
    )(order, chunks, queries, kv_rows, kv_rows, key_bias, out_weight)


def local(queries, keys, values, resid, out_weight, gain, pair_of_device, frame_of_tile):
    tok_rows, row_width = queries.shape
    head_count = row_width // HEAD
    span_rows = tok_rows // 2
    seq_count = lax.axis_size("seq")
    seq_index = lax.axis_index("seq")
    slot_frame = slot_frames(pair_of_device, frame_of_tile, 2 * seq_count)
    own_frames = lax.dynamic_slice_in_dim(slot_frame, 2 * seq_index, 2, 0).astype(jnp.int32)
    slot_count = slot_frame.shape[0]
    slot_ids = jnp.arange(slot_count, dtype=jnp.int32)
    earlier = (slot_frame[None, :] < slot_frame[:, None]) | (
        (slot_frame[None, :] == slot_frame[:, None]) & (slot_ids[None, :] < slot_ids[:, None])
    )
    rank = jnp.sum(earlier.astype(jnp.int32), axis=1)
    order = jnp.sum(
        jnp.where(rank[:, None] == slot_ids[None, :], slot_ids[:, None], 0), axis=0
    ).astype(jnp.int32)
    sorted_frame = jnp.sum(
        jnp.where(rank[:, None] == slot_ids[None, :], slot_frame[:, None], 0), axis=0
    )
    visible = jnp.sum((slot_frame[None, :] <= own_frames[:, None]).astype(jnp.int32), axis=1)
    chunks = ((visible + SLOTS_PER_CHUNK - 1) // SLOTS_PER_CHUNK).astype(jnp.int32)
    key_frame = jnp.repeat(sorted_frame.astype(jnp.int32), span_rows)
    key_bias = jnp.where(
        key_frame[None, :] <= own_frames[:, None], jnp.float32(0.0), jnp.float32(-1e30)
    ).reshape(2, 1, -1)

    kv_local = jnp.concatenate([keys, values], axis=1)
    kv_rows = lax.all_gather(kv_local, "seq", axis=0, tiled=True)
    partial = attention(queries, kv_rows, order, chunks, key_bias, out_weight)

    tp_count = lax.axis_size("tp")
    shares = lax.all_to_all(
        partial.astype(jnp.bfloat16).reshape(tp_count, tok_rows // tp_count, -1),
        "tp",
        0,
        0,
        tiled=False,
    )
    branch = jnp.sum(shares.astype(jnp.float32), axis=0)
    rms = jnp.sqrt(jnp.mean(branch * branch, axis=-1) + 1e-06)
    layer_out = resid.astype(jnp.float32) + gain[None, :] * branch / rms[:, None]
    return layer_out.astype(jnp.bfloat16)


def solution(mesh):
    in_specs = (
        P("seq", "tp"),
        P("seq", "tp"),
        P("seq", "tp"),
        P(("seq", "tp"), None),
        P("tp", None),
        P(),
        P(),
        P(),
    )
    out_specs = P(("seq", "tp"), None)
    return jax.shard_map(local, mesh=mesh, in_specs=in_specs, out_specs=out_specs, check_vma=False)
```

```python
import functools
import math

import jax
import jax.numpy as jnp
from jax import lax
from jax.experimental import pallas as pl
from jax.experimental.pallas import tpu as pltpu
from jax.sharding import PartitionSpec as P

HEAD = 128
SLOTS_PER_CHUNK = 32


def slot_frames(pair_of_device, frame_of_tile, tile_count):
    slot_ids = jnp.arange(tile_count, dtype=jnp.int32)
    paired = jnp.repeat(pair_of_device, 2)
    tile_ids = jnp.where(slot_ids % 2 == 0, paired, tile_count - 1 - paired)
    matches = tile_ids[:, None] == jnp.arange(tile_count, dtype=jnp.int32)[None, :]
    return jnp.sum(jnp.where(matches, frame_of_tile[None, :], 0), axis=1)


def attn_kernel(order_ref, chunks_ref, q_ref, k_ref, v_ref, kb_ref, o_ref, s_sc):
    tile = pl.program_id(1)
    visible = chunks_ref[tile]
    rows = q_ref.shape[0]
    span = k_ref.shape[0] // order_ref.shape[0]
    width = span * SLOTS_PER_CHUNK
    score_scale = 1.0 / math.sqrt(HEAD)
    q = q_ref[...]

    def gather(ref, c):
        pieces = []
        for m in range(SLOTS_PER_CHUNK):
            slot = order_ref[c * SLOTS_PER_CHUNK + m]
            pieces.append(ref[pl.ds(pl.multiple_of(slot * span, span), span), :])
        return jnp.concatenate(pieces, axis=0)

    def first(c, run_max):
        start = pl.multiple_of(c * width, width)
        k = gather(k_ref, c)
        s = lax.dot_general(
            q, k, (((1,), (1,)), ((), ())), preferred_element_type=jnp.float32
        ) * score_scale
        masked = s + kb_ref[:, pl.ds(start, width)]
        s_sc[:, pl.ds(start, width)] = masked
        return jnp.maximum(run_max, jnp.max(masked, axis=1, keepdims=True))

    row_max = lax.fori_loop(0, visible, first, jnp.full((rows, 1), -1e30, jnp.float32))

    def second(c, carry):
        totals, acc = carry
        start = pl.multiple_of(c * width, width)
        probs = jnp.exp(s_sc[:, pl.ds(start, width)] - row_max)
        totals = totals + jnp.sum(probs, axis=1, keepdims=True)
        v = gather(v_ref, c)
        acc = acc + jnp.dot(probs.astype(jnp.bfloat16), v, preferred_element_type=jnp.float32)
        return totals, acc

    totals, acc = lax.fori_loop(
        0,
        visible,
        second,
        (jnp.zeros((rows, 1), jnp.float32), jnp.zeros((rows, HEAD), jnp.float32)),
    )
    o_ref[...] = (acc / totals).astype(o_ref.dtype)


def attention(queries, kv_rows, order, chunks, key_bias):
    tok_rows = queries.shape[0]
    tile_rows = tok_rows // 2
    key_count = kv_rows.shape[0]
    head_count = queries.shape[1] // HEAD
    cost = pl.CostEstimate(
        flops=2 * tok_rows * key_count * HEAD * head_count,
        transcendentals=tok_rows * key_count * head_count // 2,
        bytes_accessed=(key_count * 2 * HEAD * 2 + tok_rows * HEAD * 4) * head_count,
    )
    return pl.pallas_call(
        attn_kernel,
        out_shape=jax.ShapeDtypeStruct((tok_rows, head_count * HEAD), jnp.bfloat16),
        grid_spec=pltpu.PrefetchScalarGridSpec(
            num_scalar_prefetch=2,
            grid=(head_count, 2),
            in_specs=[
                pl.BlockSpec((tile_rows, HEAD), lambda h, i, o, c: (i, h)),
                pl.BlockSpec((key_count, HEAD), lambda h, i, o, c: (0, h)),
                pl.BlockSpec((key_count, HEAD), lambda h, i, o, c: (0, head_count + h)),
                pl.BlockSpec((None, 1, key_count), lambda h, i, o, c: (i, 0, 0)),
            ],
            out_specs=pl.BlockSpec((tile_rows, HEAD), lambda h, i, o, c: (i, h)),
            scratch_shapes=[pltpu.VMEM((tile_rows, key_count), jnp.float32)],
        ),
        compiler_params=pltpu.CompilerParams(vmem_limit_bytes=56 * 1024 * 1024),
        cost_estimate=cost,
    )(order, chunks, queries, kv_rows, kv_rows, key_bias)


def local(queries, keys, values, resid, out_weight, gain, pair_of_device, frame_of_tile):
    tok_rows, row_width = queries.shape
    head_count = row_width // HEAD
    span_rows = tok_rows // 2
    seq_count = lax.axis_size("seq")
    seq_index = lax.axis_index("seq")
    slot_frame = slot_frames(pair_of_device, frame_of_tile, 2 * seq_count)
    own_frames = lax.dynamic_slice_in_dim(slot_frame, 2 * seq_index, 2, 0).astype(jnp.int32)
    slot_count = slot_frame.shape[0]
    slot_ids = jnp.arange(slot_count, dtype=jnp.int32)
    earlier = (slot_frame[None, :] < slot_frame[:, None]) | (
        (slot_frame[None, :] == slot_frame[:, None]) & (slot_ids[None, :] < slot_ids[:, None])
    )
    rank = jnp.sum(earlier.astype(jnp.int32), axis=1)
    order = jnp.sum(
        jnp.where(rank[:, None] == slot_ids[None, :], slot_ids[:, None], 0), axis=0
    ).astype(jnp.int32)
    sorted_frame = jnp.sum(
        jnp.where(rank[:, None] == slot_ids[None, :], slot_frame[:, None], 0), axis=0
    )
    visible = jnp.sum((slot_frame[None, :] <= own_frames[:, None]).astype(jnp.int32), axis=1)
    chunks = ((visible + SLOTS_PER_CHUNK - 1) // SLOTS_PER_CHUNK).astype(jnp.int32)
    key_frame = jnp.repeat(sorted_frame.astype(jnp.int32), span_rows)
    key_bias = jnp.where(
        key_frame[None, :] <= own_frames[:, None], jnp.float32(0.0), jnp.float32(-1e30)
    ).reshape(2, 1, -1)

    kv_local = jnp.concatenate([keys, values], axis=1)
    kv_rows = lax.all_gather(kv_local, "seq", axis=0, tiled=True)
    attn = attention(queries, kv_rows, order, chunks, key_bias)
    partial = jnp.dot(attn, out_weight, preferred_element_type=jnp.float32)

    tp_count = lax.axis_size("tp")
    shares = lax.all_to_all(
        partial.astype(jnp.bfloat16).reshape(tp_count, tok_rows // tp_count, -1),
        "tp",
        0,
        0,
        tiled=False,
    )
    branch = jnp.sum(shares.astype(jnp.float32), axis=0)
    rms = jnp.sqrt(jnp.mean(branch * branch, axis=-1) + 1e-06)
    layer_out = resid.astype(jnp.float32) + gain[None, :] * branch / rms[:, None]
    return layer_out.astype(jnp.bfloat16)


def solution(mesh):
    in_specs = (
        P("seq", "tp"),
        P("seq", "tp"),
        P("seq", "tp"),
        P(("seq", "tp"), None),
        P("tp", None),
        P(),
        P(),
        P(),
    )
    out_specs = P(("seq", "tp"), None)
    return jax.shard_map(local, mesh=mesh, in_specs=in_specs, out_specs=out_specs, check_vma=False)
```
